256 devices in a mesh: blk: 64 (over x, z, core), st: 4 (over y).
Axes of the slice: x: 4, y: 4, z: 8, core: 2. Of those that a mesh axis runs over, the one named last changes fastest.
Arguments:
- field: bfloat16 [65536, 2048], P('blk', 'st'), may hold values from -6 to 6
- storm_cov: bfloat16 [2048, 2048], P('st')
- order: int32 [512], replicated, may hold values from 0 to 511, each once
- neighbours: int32 [512, 6], replicated, may hold values from 0 to 511, as said below
- coeffs: bfloat16 [512, 6, 128, 128], P('blk'), may hold values from -0.3125 to 0.3125
- inv_factors: bfloat16 [512, 128, 128], P('blk')
Outputs:
- whitened: bfloat16 [65536, 2048], P('blk', 'st')
- product: bfloat16 [65536, 2048], P('blk', 'st')
The draws below stay inside these ranges and needn't reach their ends.
Inputs may be any that keep to these rules, and one draw needn't show every extreme that they name: `neighbours`: block n belongs to owner n // 8, and owners are counted modulo the number of owners. Every entry of a block's row names a block whose owner lies within 3 owners of the block's own owner, on either side. Among the 48 entries of the rows of one owner's blocks, at most 7 name blocks of any one owner, and exactly 7 name blocks of some owner, for every owner.
All inputs are finite; a program needn't handle non-finite values.
Results may differ from the reference program's by a relative error of at most 0.007.
Values may be sent and summed in bfloat16 or wider, within the bound.
No kernel may reach another device: no remote copies, remote signals or barrier semaphores. Data moves between devices by JAX's collectives and lax.ppermute only.
A program may use at most 128 MiB of HBM per device.

```python
import jax
import jax.numpy as jnp
from jax import lax

S = 2048
BS = 128
NNB = 6
REACH = 3
BLK_DEV = 8
NB = 512
NODES = 65536


def draw_storm_cov(key, part):
    first = jax.random.fold_in(key, 0)
    raw = jax.random.normal(first, (S, S), jnp.float32)
    sym = (raw + jnp.transpose(raw)) * (0.7071068 / S ** 0.5)
    return sym.astype(jnp.bfloat16)


def draw_inv_factors(key, part):
    first, second = jax.random.split(key)
    row_ids = jnp.arange(BS)
    below = row_ids[:, None] > row_ids[None, :]
    diagonal_cells = row_ids[:, None] == row_ids[None, :]
    spread = jax.random.normal(first, (NB, BS, BS), jnp.float32)
    diag_vals = jax.random.uniform(second, (NB, BS), jnp.float32, 0.6, 1.4)
    lower = jnp.where(below, spread * (0.6 / BS ** 0.5), 0.0)
    matrix = lower + jnp.where(diagonal_cells, diag_vals[:, :, None], 0.0)
    return matrix.astype(jnp.bfloat16)


def draw_neighbours(key, part):
    devices = NB // BLK_DEV
    span = 2 * REACH + 1
    slot_count = NNB * BLK_DEV
    capacity = (slot_count + span - 1) // span
    first, second = jax.random.split(jax.random.fold_in(key, 17))
    device_keys = jax.random.split(first, devices)
    shuffles = jax.vmap(lambda one_key: jax.random.permutation(one_key, span))(device_keys).astype(jnp.int32)
    group_ids = jnp.arange(slot_count) // capacity
    offsets = shuffles[:, group_ids] - REACH
    sources = (jnp.arange(devices, dtype=jnp.int32)[:, None] + offsets + devices) % devices
    rolls = jax.random.randint(second, (devices, slot_count), 0, 256, jnp.int32)
    local_ids = rolls * rolls * BLK_DEV // 65536
    return (sources * BLK_DEV + local_ids).reshape(NB, NNB).astype(jnp.int32)


def levels(stream_key, dims, cuts, low, top_value):
    loudness, own = 1.0, jax.random.fold_in(stream_key, 6)
    for dim, shards_of in cuts:
        heights = jnp.exp(jax.random.uniform(jax.random.fold_in(own, dim), (shards_of,), jnp.float32, low / len(cuts), top_value / len(cuts)))
        loudness = loudness * jnp.repeat(heights, dims[dim] // shards_of).reshape([-1 if axis == dim else 1 for axis in range(len(dims))])
    return loudness


def centred(key, dims, deviation, most, cuts=(), kind=jnp.bfloat16):
    drawn = jax.random.normal(key, dims, jnp.float32) * deviation
    if len(cuts) > 0:
        drawn = levels(key, dims, cuts, -0.22, 0.18) * drawn
    return jnp.clip(drawn, min=-most, max=most).astype(kind)


def setup_inputs(seed: int = 0) -> dict:
    key_list = jax.random.split(jax.random.key(seed), 7)
    field = centred(key_list[0], (NODES, S), 1.0, 6.0, ((0, 64), (1, 4)))
    storm_cov = draw_storm_cov(jax.random.fold_in(key_list[6], 71), 0)
    order = jax.random.permutation(key_list[2], NB).astype(jnp.int32)
    neighbours = draw_neighbours(jax.random.fold_in(key_list[6], 71), 0)
    coeffs = centred(key_list[4], (NB, NNB, BS, BS), (3 * BS) ** -0.5, 0.3125, ((0, 64),))
    inv_factors = draw_inv_factors(jax.random.fold_in(key_list[6], 71), 0)
    return {"field": field, "storm_cov": storm_cov, "order": order, "neighbours": neighbours, "coeffs": coeffs, "inv_factors": inv_factors}


def reference(field, storm_cov, order, neighbours, coeffs, inv_factors):
    mixed = jnp.dot(field, storm_cov, preferred_element_type=jnp.float32).astype(jnp.bfloat16)
    blocks = mixed.reshape(NB, BS, S)
    usable = order[neighbours] < order[:, None]
    masked = jnp.where(usable[:, :, None, None], coeffs, jnp.zeros((), jnp.bfloat16))

    def advance(total, position):
        listed = neighbours[position]
        nearby = blocks[listed].astype(jnp.float32)
        weights = masked[position].astype(jnp.float32)
        pulled = jnp.einsum("jpq,jqs->ps", weights, nearby)
        conditioned = (blocks[position].astype(jnp.float32) - pulled).astype(jnp.bfloat16)
        factor = inv_factors[position]
        whitened = jnp.dot(factor, conditioned, preferred_element_type=jnp.float32).astype(jnp.bfloat16)
        lifted = jnp.dot(jnp.transpose(factor), whitened, preferred_element_type=jnp.float32)
        lifted_half = lax.optimization_barrier(lifted.astype(jnp.bfloat16)).astype(jnp.float32)
        returned = (-jnp.einsum("jqp,qs->jps", weights, lifted_half)).astype(jnp.bfloat16)
        total = total.at[position].add(lifted)
        total = total.at[listed].add(returned.astype(jnp.float32))
        return total, whitened

    total, whitened = lax.scan(advance, jnp.zeros((NB, BS, S), jnp.float32), jnp.arange(NB, dtype=jnp.int32))
    return whitened.reshape(NODES, S), total.astype(jnp.bfloat16).reshape(NODES, S)
```

```python
import jax
import jax.numpy as jnp
from jax import lax
from jax.experimental import pallas as pl
from jax.experimental.pallas import tpu as pltpu
from jax.sharding import PartitionSpec as P

REACH = 3
CHUNKS = 1


def from_behind(array, axis, by):
    count = lax.axis_size(axis)
    return lax.ppermute(array, axis, [(i, (i + by) % count) for i in range(count)])


def accumulate_kernel(target_ref, lifted_ref, back_ref, out_ref, total_ref):
    total_ref[...] = lifted_ref[...]

    def body(slot, carry):
        target = target_ref[slot]

        @pl.when(target >= 0)
        def _():
            total_ref[target] = total_ref[target] + back_ref[slot].astype(jnp.float32)

        return carry

    lax.fori_loop(0, back_ref.shape[0], body, 0)
    out_ref[...] = total_ref[...].astype(out_ref.dtype)


def accumulate(target, lifted, back):
    blocks, rows, width = lifted.shape
    slots = back.shape[0]
    return pl.pallas_call(
        accumulate_kernel,
        out_shape=jax.ShapeDtypeStruct(lifted.shape, jnp.bfloat16),
        in_specs=[
            pl.BlockSpec(memory_space=pltpu.SMEM),
            pl.BlockSpec(memory_space=pltpu.VMEM),
            pl.BlockSpec(memory_space=pltpu.VMEM),
        ],
        out_specs=pl.BlockSpec(memory_space=pltpu.VMEM),
        scratch_shapes=[pltpu.VMEM(lifted.shape, jnp.float32)],
        cost_estimate=pl.CostEstimate(
            flops=slots * rows * width,
            bytes_accessed=blocks * rows * width * 6 + slots * rows * width * 2,
            transcendentals=0,
        ),
    )(target, lifted, back)


def local(field, storm_cov, order, neighbours, coeffs, inv_factors):
    node_rows, storm_cols = field.shape
    per_device, near_count, block_size, _ = coeffs.shape
    devices = lax.axis_size("blk")
    storm_parts = lax.axis_size("st")
    device = lax.axis_index("blk")
    slot_count = near_count * per_device
    span = 2 * REACH + 1
    capacity = (slot_count + span - 1) // span

    field_all = lax.all_gather(field, "st", axis=1, tiled=True)
    cov_split = storm_cov.reshape(storm_cov.shape[0], storm_parts, storm_cols)
    cov_split = jnp.transpose(cov_split, (1, 0, 2))
    cov_cols = lax.all_to_all(cov_split, "st", 0, 0, tiled=True)
    cov_cols = cov_cols.reshape(storm_parts * storm_cov.shape[0], storm_cols)

    listed = neighbours.reshape(devices, slot_count)
    owners = listed // per_device
    local_all = listed - owners * per_device
    earlier = jnp.tril(jnp.ones((slot_count, slot_count), jnp.bool_), -1)
    same_owner = owners[:, :, None] == owners[:, None, :]
    ordinal = jnp.sum(same_owner & earlier[None], axis=2)
    my_owners = lax.dynamic_index_in_dim(owners, device, 0, keepdims=False)
    my_rank = lax.dynamic_index_in_dim(ordinal, device, 0, keepdims=False)
    gap = (device - my_owners + devices) % devices
    step_of = jnp.where(gap <= REACH, gap, gap - devices)
    cap_ids = jnp.arange(capacity, dtype=jnp.int32)
    pickers = []
    targets = []
    for step in range(-REACH, REACH + 1):
        reader = (device + step + devices) % devices
        reader_owners = lax.dynamic_index_in_dim(owners, reader, 0, keepdims=False)
        reader_rank = lax.dynamic_index_in_dim(ordinal, reader, 0, keepdims=False)
        reader_local = lax.dynamic_index_in_dim(local_all, reader, 0, keepdims=False)
        chosen = (reader_owners == device)[None, :] & (reader_rank[None, :] == cap_ids[:, None])
        used = jnp.any(chosen, axis=1)
        picked = jnp.sum(jnp.where(chosen, reader_local[None, :], 0), axis=1)
        pickers.append(picked)
        targets.append(jnp.where(used, picked, -1))
    all_targets = jnp.concatenate(targets, axis=0)
    source_ids = jnp.arange(span * capacity, dtype=jnp.int32)
    my_slot = (step_of + REACH) * capacity + my_rank
    entry_ids = jnp.arange(slot_count, dtype=jnp.int32)
    slot_entry = jnp.sum(
        jnp.where(my_slot[None, :] == source_ids[:, None], entry_ids[None, :], 0), axis=1
    )

    mine_listed = lax.dynamic_slice_in_dim(neighbours, device * per_device, per_device, 0)
    block_ids = jnp.arange(order.shape[0], dtype=jnp.int32)
    nbr_order = jnp.sum(jnp.where(mine_listed[:, :, None] == block_ids, order, 0), axis=2)
    own_order = lax.dynamic_slice_in_dim(order, device * per_device, per_device, 0)
    usable = nbr_order < own_order[:, None]
    masked = jnp.where(usable[:, :, None, None], coeffs, jnp.zeros((), jnp.bfloat16))

    width = storm_cols // CHUNKS
    whitened_parts = []
    product_parts = []
    for chunk in range(CHUNKS):
        cols = cov_cols[:, chunk * width : (chunk + 1) * width]
        mixed = jnp.dot(field_all, cols, preferred_element_type=jnp.float32).astype(jnp.bfloat16)
        own_blocks = mixed.reshape(per_device, block_size, width)
        arrivals = []
        for step in range(-REACH, REACH + 1):
            outgoing = jnp.take(own_blocks, pickers[step + REACH], axis=0)
            if step != 0:
                outgoing = from_behind(outgoing, "blk", step)
            arrivals.append(outgoing)
        incoming = jnp.concatenate(arrivals, axis=0)
        near_rows = jnp.take(incoming, my_slot, axis=0)
        near_rows = near_rows.reshape(per_device, near_count, block_size, width)
        pulled = jnp.einsum(
            "ijpq,ijqs->ips", masked, near_rows, preferred_element_type=jnp.float32
        )
        conditioned = (own_blocks.astype(jnp.float32) - pulled).astype(jnp.bfloat16)
        whitened = jnp.einsum(
            "ipq,iqs->ips", inv_factors, conditioned, preferred_element_type=jnp.float32
        ).astype(jnp.bfloat16)
        lifted = jnp.einsum(
            "iqp,iqs->ips", inv_factors, whitened, preferred_element_type=jnp.float32
        )
        lifted_half = lifted.astype(jnp.bfloat16)
        returned = (
            -jnp.einsum("ijqp,iqs->ijps", masked, lifted_half, preferred_element_type=jnp.float32)
        ).astype(jnp.bfloat16)
        returned = returned.reshape(slot_count, block_size, width)
        returned_out = jnp.take(returned, slot_entry, axis=0)
        backs = []
        for step in range(-REACH, REACH + 1):
            piece = returned_out[(step + REACH) * capacity : (step + REACH + 1) * capacity]
            if step != 0:
                piece = from_behind(piece, "blk", -step)
            backs.append(piece)
        back = jnp.concatenate(backs, axis=0)
        product = accumulate(all_targets, lifted, back)
        whitened_parts.append(whitened.reshape(node_rows, width))
        product_parts.append(product.reshape(node_rows, width))
    if CHUNKS == 1:
        return whitened_parts[0], product_parts[0]
    return jnp.concatenate(whitened_parts, axis=1), jnp.concatenate(product_parts, axis=1)


def solution(mesh):
    in_specs = (
        P("blk", "st"),
        P("st", None),
        P(),
        P(),
        P("blk", None, None, None),
        P("blk", None, None),
    )
    out_specs = (P("blk", "st"), P("blk", "st"))
    return jax.shard_map(local, mesh=mesh, in_specs=in_specs, out_specs=out_specs, check_vma=False)
```

```python
import jax
import jax.numpy as jnp
from jax import lax
from jax.experimental import pallas as pl
from jax.experimental.pallas import tpu as pltpu
from jax.sharding import PartitionSpec as P

REACH = 3
CHUNKS = 1


def from_behind(array, axis, by):
    count = lax.axis_size(axis)
    return lax.ppermute(array, axis, [(i, (i + by) % count) for i in range(count)])


def accumulate_kernel(target_ref, lifted_ref, back_ref, out_ref, total_ref):
    total_ref[...] = lifted_ref[...]

    def body(slot, carry):
        target = target_ref[slot]

        @pl.when(target >= 0)
        def _():
            total_ref[target] = total_ref[target] + back_ref[slot].astype(jnp.float32)

        return carry

    lax.fori_loop(0, back_ref.shape[0], body, 0)
    out_ref[...] = total_ref[...].astype(out_ref.dtype)


def accumulate(target, lifted, back):
    blocks, rows, width = lifted.shape
    slots = back.shape[0]
    return pl.pallas_call(
        accumulate_kernel,
        out_shape=jax.ShapeDtypeStruct(lifted.shape, jnp.bfloat16),
        in_specs=[
            pl.BlockSpec(memory_space=pltpu.SMEM),
            pl.BlockSpec(memory_space=pltpu.VMEM),
            pl.BlockSpec(memory_space=pltpu.VMEM),
        ],
        out_specs=pl.BlockSpec(memory_space=pltpu.VMEM),
        scratch_shapes=[pltpu.VMEM(lifted.shape, jnp.float32)],
        cost_estimate=pl.CostEstimate(
            flops=slots * rows * width,
            bytes_accessed=blocks * rows * width * 6 + slots * rows * width * 2,
            transcendentals=0,
        ),
    )(target, lifted, back)


def local(field, storm_cov, order, neighbours, coeffs, inv_factors):
    node_rows, storm_cols = field.shape
    per_device, near_count, block_size, _ = coeffs.shape
    devices = lax.axis_size("blk")
    device = lax.axis_index("blk")
    slot_count = near_count * per_device
    span = 2 * REACH + 1
    capacity = (slot_count + span - 1) // span

    field_all = lax.all_gather(field, "st", axis=1, tiled=True)

    listed = neighbours.reshape(devices, slot_count)
    owners = listed // per_device
    local_all = listed - owners * per_device
    earlier = jnp.tril(jnp.ones((slot_count, slot_count), jnp.bool_), -1)
    same_owner = owners[:, :, None] == owners[:, None, :]
    ordinal = jnp.sum(same_owner & earlier[None], axis=2)
    my_owners = lax.dynamic_index_in_dim(owners, device, 0, keepdims=False)
    my_rank = lax.dynamic_index_in_dim(ordinal, device, 0, keepdims=False)
    gap = (device - my_owners + devices) % devices
    step_of = jnp.where(gap <= REACH, gap, gap - devices)
    cap_ids = jnp.arange(capacity, dtype=jnp.int32)
    pickers = []
    targets = []
    for step in range(-REACH, REACH + 1):
        reader = (device + step + devices) % devices
        reader_owners = lax.dynamic_index_in_dim(owners, reader, 0, keepdims=False)
        reader_rank = lax.dynamic_index_in_dim(ordinal, reader, 0, keepdims=False)
        reader_local = lax.dynamic_index_in_dim(local_all, reader, 0, keepdims=False)
        chosen = (reader_owners == device)[None, :] & (reader_rank[None, :] == cap_ids[:, None])
        used = jnp.any(chosen, axis=1)
        picked = jnp.sum(jnp.where(chosen, reader_local[None, :], 0), axis=1)
        pickers.append(picked)
        targets.append(jnp.where(used, picked, -1))
    all_targets = jnp.concatenate(targets, axis=0)
    source_ids = jnp.arange(span * capacity, dtype=jnp.int32)
    my_slot = (step_of + REACH) * capacity + my_rank
    entry_ids = jnp.arange(slot_count, dtype=jnp.int32)
    slot_entry = jnp.sum(
        jnp.where(my_slot[None, :] == source_ids[:, None], entry_ids[None, :], 0), axis=1
    )

    mine_listed = lax.dynamic_slice_in_dim(neighbours, device * per_device, per_device, 0)
    block_ids = jnp.arange(order.shape[0], dtype=jnp.int32)
    nbr_order = jnp.sum(jnp.where(mine_listed[:, :, None] == block_ids, order, 0), axis=2)
    own_order = lax.dynamic_slice_in_dim(order, device * per_device, per_device, 0)
    usable = nbr_order < own_order[:, None]
    masked = jnp.where(usable[:, :, None, None], coeffs, jnp.zeros((), jnp.bfloat16))

    width = storm_cols // CHUNKS
    whitened_parts = []
    product_parts = []
    for chunk in range(CHUNKS):
        rows = storm_cov[chunk * width : (chunk + 1) * width]
        mixed = lax.dot_general(
            field_all, rows, (((1,), (1,)), ((), ())), preferred_element_type=jnp.float32
        ).astype(jnp.bfloat16)
        own_blocks = mixed.reshape(per_device, block_size, width)
        arrivals = []
        for step in range(-REACH, REACH + 1):
            outgoing = jnp.take(own_blocks, pickers[step + REACH], axis=0)
            if step != 0:
                outgoing = from_behind(outgoing, "blk", step)
            arrivals.append(outgoing)
        incoming = jnp.concatenate(arrivals, axis=0)
        near_rows = jnp.take(incoming, my_slot, axis=0)
        near_rows = near_rows.reshape(per_device, near_count, block_size, width)
        pulled = jnp.einsum(
            "ijpq,ijqs->ips", masked, near_rows, preferred_element_type=jnp.float32
        )
        conditioned = (own_blocks.astype(jnp.float32) - pulled).astype(jnp.bfloat16)
        whitened = jnp.einsum(
            "ipq,iqs->ips", inv_factors, conditioned, preferred_element_type=jnp.float32
        ).astype(jnp.bfloat16)
        lifted = jnp.einsum(
            "iqp,iqs->ips", inv_factors, whitened, preferred_element_type=jnp.float32
        )
        lifted_half = lifted.astype(jnp.bfloat16)
        returned = (
            -jnp.einsum("ijqp,iqs->ijps", masked, lifted_half, preferred_element_type=jnp.float32)
        ).astype(jnp.bfloat16)
        returned = returned.reshape(slot_count, block_size, width)
        backs = []
        for step in range(-REACH, REACH + 1):
            piece = jnp.take(
                returned, slot_entry[(step + REACH) * capacity : (step + REACH + 1) * capacity], axis=0
            )
            if step != 0:
                piece = from_behind(piece, "blk", -step)
            backs.append(piece)
        back = jnp.concatenate(backs, axis=0)
        product = accumulate(all_targets, lifted, back)
        whitened_parts.append(whitened.reshape(node_rows, width))
        product_parts.append(product.reshape(node_rows, width))
    if CHUNKS == 1:
        return whitened_parts[0], product_parts[0]
    return jnp.concatenate(whitened_parts, axis=1), jnp.concatenate(product_parts, axis=1)


def solution(mesh):
    in_specs = (
        P("blk", "st"),
        P("st", None),
        P(),
        P(),
        P("blk", None, None, None),
        P("blk", None, None),
    )
    out_specs = (P("blk", "st"), P("blk", "st"))
    return jax.shard_map(local, mesh=mesh, in_specs=in_specs, out_specs=out_specs, check_vma=False)
```

```python
import jax
import jax.numpy as jnp
from jax import lax
from jax.experimental import pallas as pl
from jax.experimental.pallas import tpu as pltpu
from jax.sharding import PartitionSpec as P

REACH = 3
CHUNKS = 1


def from_behind(array, axis, by):
    count = lax.axis_size(axis)
    return lax.ppermute(array, axis, [(i, (i + by) % count) for i in range(count)])


def local_kernel(step_ref, index_ref, *refs):
    sources = list(refs[:7])
    masked_ref, masked_t_ref, inv_ref, inv_t_ref = refs[7:11]
    whitened_ref, total_ref = refs[11:13]
    pieces = list(refs[13:19])
    pieces.insert(3, None)
    pulled_ref, half_ref = refs[19:21]
    own_ref = sources[3]
    near_count = masked_ref.shape[1]
    entries = masked_ref.shape[0] * near_count
    pulled_ref[...] = jnp.zeros(pulled_ref.shape, jnp.float32)

    def pull(entry, carry):
        block = entry // near_count
        slot = entry % near_count
        step = step_ref[entry]
        index = index_ref[entry]
        weights = masked_ref[block, slot]
        for k, source in enumerate(sources):

            @pl.when(step == k)
            def _():
                pulled_ref[block] = pulled_ref[block] + jnp.dot(
                    weights, source[index], preferred_element_type=jnp.float32
                )

        return carry

    lax.fori_loop(0, entries, pull, 0)

    def whiten(block, carry):
        conditioned = (own_ref[block].astype(jnp.float32) - pulled_ref[block]).astype(jnp.bfloat16)
        whitened = jnp.dot(
            inv_ref[block], conditioned, preferred_element_type=jnp.float32
        ).astype(jnp.bfloat16)
        whitened_ref[block] = whitened
        lifted = jnp.dot(inv_t_ref[block], whitened, preferred_element_type=jnp.float32)
        total_ref[block] = lifted
        half_ref[block] = lifted.astype(jnp.bfloat16)
        return carry

    lax.fori_loop(0, masked_ref.shape[0], whiten, 0)

    def give_back(entry, carry):
        block = entry // near_count
        slot = entry % near_count
        step = step_ref[entry]
        index = index_ref[entry]
        returned = (
            -jnp.dot(masked_t_ref[block, slot], half_ref[block], preferred_element_type=jnp.float32)
        ).astype(jnp.bfloat16)
        for k, piece in enumerate(pieces):

            @pl.when(step == k)
            def _():
                if piece is None:
                    total_ref[index] = total_ref[index] + returned.astype(jnp.float32)
                else:
                    piece[index] = returned

        return carry

    lax.fori_loop(0, entries, give_back, 0)


def local_stage(step_table, index_table, sources, masked, masked_t, inv, inv_t):
    own = sources[3]
    blocks, rows, width = own.shape
    piece_shape = sources[0].shape
    entries = masked.shape[0] * masked.shape[1]
    vmem = pl.BlockSpec(memory_space=pltpu.VMEM)
    smem = pl.BlockSpec(memory_space=pltpu.SMEM)
    return pl.pallas_call(
        local_kernel,
        out_shape=[
            jax.ShapeDtypeStruct(own.shape, jnp.bfloat16),
            jax.ShapeDtypeStruct(own.shape, jnp.float32),
        ]
        + [jax.ShapeDtypeStruct(piece_shape, jnp.bfloat16)] * 6,
        in_specs=[smem, smem] + [vmem] * 11,
        out_specs=[vmem] * 8,
        scratch_shapes=[
            pltpu.VMEM(own.shape, jnp.float32),
            pltpu.VMEM(own.shape, jnp.bfloat16),
        ],
        compiler_params=pltpu.CompilerParams(vmem_limit_bytes=56 * 1024 * 1024),
        cost_estimate=pl.CostEstimate(
            flops=2 * rows * rows * width * (2 * entries + 2 * blocks),
            bytes_accessed=2 * (2 * own.size + 12 * sources[0].size) + 8 * own.size,
            transcendentals=0,
        ),
    )(step_table, index_table, *sources, masked, masked_t, inv, inv_t)


def accumulate_kernel(target_ref, lifted_ref, *refs):
    pieces = refs[:6]
    out_ref, total_ref = refs[6:8]
    capacity = pieces[0].shape[0]
    total_ref[...] = lifted_ref[...]
    for k, piece in enumerate(pieces):

        def body(slot, carry, k=k, piece=piece):
            target = target_ref[k * capacity + slot]

            @pl.when(target >= 0)
            def _():
                total_ref[target] = total_ref[target] + piece[slot].astype(jnp.float32)

            return carry

        lax.fori_loop(0, capacity, body, 0)
    out_ref[...] = total_ref[...].astype(out_ref.dtype)


def accumulate(target, total, pieces):
    blocks, rows, width = total.shape
    vmem = pl.BlockSpec(memory_space=pltpu.VMEM)
    return pl.pallas_call(
        accumulate_kernel,
        out_shape=jax.ShapeDtypeStruct(total.shape, jnp.bfloat16),
        in_specs=[pl.BlockSpec(memory_space=pltpu.SMEM), vmem] + [vmem] * 6,
        out_specs=vmem,
        scratch_shapes=[pltpu.VMEM(total.shape, jnp.float32)],
        compiler_params=pltpu.CompilerParams(vmem_limit_bytes=56 * 1024 * 1024),
        cost_estimate=pl.CostEstimate(
            flops=6 * pieces[0].size,
            bytes_accessed=6 * total.size + 12 * pieces[0].size,
            transcendentals=0,
        ),
    )(target, total, *pieces)


def local(field, storm_cov, order, neighbours, coeffs, inv_factors):
    node_rows, storm_cols = field.shape
    per_device, near_count, block_size, _ = coeffs.shape
    devices = lax.axis_size("blk")
    device = lax.axis_index("blk")
    slot_count = near_count * per_device
    span = 2 * REACH + 1
    capacity = (slot_count + span - 1) // span

    field_all = lax.all_gather(field, "st", axis=1, tiled=True)

    listed = neighbours.reshape(devices, slot_count)
    owners = listed // per_device
    local_all = listed - owners * per_device
    earlier = jnp.tril(jnp.ones((slot_count, slot_count), jnp.bool_), -1)
    same_owner = owners[:, :, None] == owners[:, None, :]
    ordinal = jnp.sum(same_owner & earlier[None], axis=2)
    my_owners = lax.dynamic_index_in_dim(owners, device, 0, keepdims=False)
    my_rank = lax.dynamic_index_in_dim(ordinal, device, 0, keepdims=False)
    gap = (device - my_owners + devices) % devices
    step_of = jnp.where(gap <= REACH, gap, gap - devices)
    cap_ids = jnp.arange(capacity, dtype=jnp.int32)
    my_local = lax.dynamic_index_in_dim(local_all, device, 0, keepdims=False)
    step_table = step_of + REACH
    index_table = jnp.where(step_of == 0, my_local, my_rank)
    pickers = []
    targets = []
    for step in range(-REACH, REACH + 1):
        if step == 0:
            continue
        reader = (device + step + devices) % devices
        reader_owners = lax.dynamic_index_in_dim(owners, reader, 0, keepdims=False)
        reader_rank = lax.dynamic_index_in_dim(ordinal, reader, 0, keepdims=False)
        reader_local = lax.dynamic_index_in_dim(local_all, reader, 0, keepdims=False)
        chosen = (reader_owners == device)[None, :] & (reader_rank[None, :] == cap_ids[:, None])
        used = jnp.any(chosen, axis=1)
        picked = jnp.sum(jnp.where(chosen, reader_local[None, :], 0), axis=1)
        pickers.append(picked)
        targets.append(jnp.where(used, picked, -1))
    all_targets = jnp.concatenate(targets, axis=0)
    source_ids = jnp.arange(span * capacity, dtype=jnp.int32)
    my_slot = (step_of + REACH) * capacity + my_rank
    entry_ids = jnp.arange(slot_count, dtype=jnp.int32)
    slot_entry = jnp.sum(
        jnp.where(my_slot[None, :] == source_ids[:, None], entry_ids[None, :], 0), axis=1
    )

    mine_listed = lax.dynamic_slice_in_dim(neighbours, device * per_device, per_device, 0)
    block_ids = jnp.arange(order.shape[0], dtype=jnp.int32)
    nbr_order = jnp.sum(jnp.where(mine_listed[:, :, None] == block_ids, order, 0), axis=2)
    own_order = lax.dynamic_slice_in_dim(order, device * per_device, per_device, 0)
    usable = nbr_order < own_order[:, None]
    masked = jnp.where(usable[:, :, None, None], coeffs, jnp.zeros((), jnp.bfloat16))
    masked_t = jnp.swapaxes(masked, 2, 3)
    inv_t = jnp.swapaxes(inv_factors, 1, 2)

    width = storm_cols // CHUNKS
    whitened_parts = []
    product_parts = []
    for chunk in range(CHUNKS):
        rows = storm_cov[chunk * width : (chunk + 1) * width]
        mixed = lax.dot_general(
            field_all, rows, (((1,), (1,)), ((), ())), preferred_element_type=jnp.float32
        ).astype(jnp.bfloat16)
        own_blocks = mixed.reshape(per_device, block_size, width)
        sources = []
        for k, step in enumerate([s for s in range(-REACH, REACH + 1) if s != 0]):
            outgoing = jnp.take(own_blocks, pickers[k], axis=0)
            sources.append(from_behind(outgoing, "blk", step))
        sources.insert(REACH, own_blocks)
        outs = local_stage(step_table, index_table, sources, masked, masked_t, inv_factors, inv_t)
        whitened, total = outs[0], outs[1]
        backs = []
        for k, step in enumerate([s for s in range(-REACH, REACH + 1) if s != 0]):
            backs.append(from_behind(outs[2 + k], "blk", -step))
        product = accumulate(all_targets, total, backs)
        whitened_parts.append(whitened.reshape(node_rows, width))
        product_parts.append(product.reshape(node_rows, width))
    if CHUNKS == 1:
        return whitened_parts[0], product_parts[0]
    return jnp.concatenate(whitened_parts, axis=1), jnp.concatenate(product_parts, axis=1)


def solution(mesh):
    in_specs = (
        P("blk", "st"),
        P("st", None),
        P(),
        P(),
        P("blk", None, None, None),
        P("blk", None, None),
    )
    out_specs = (P("blk", "st"), P("blk", "st"))
    return jax.shard_map(local, mesh=mesh, in_specs=in_specs, out_specs=out_specs, check_vma=False)
```

```python
import jax
import jax.numpy as jnp
from jax import lax
from jax.experimental import pallas as pl
from jax.experimental.pallas import tpu as pltpu
from jax.sharding import PartitionSpec as P

REACH = 3
CHUNKS = 2


def from_behind(array, axis, by):
    count = lax.axis_size(axis)
    return lax.ppermute(array, axis, [(i, (i + by) % count) for i in range(count)])


def pick_kernel(table_ref, own_ref, *pieces):
    capacity = pieces[0].shape[0]
    for k, piece in enumerate(pieces):

        def body(slot, carry, k=k, piece=piece):
            piece[slot] = own_ref[table_ref[k * capacity + slot]]
            return carry

        lax.fori_loop(0, capacity, body, 0)


def pick(table, own, capacity, count):
    blocks, rows, width = own.shape
    vmem = pl.BlockSpec(memory_space=pltpu.VMEM)
    return pl.pallas_call(
        pick_kernel,
        out_shape=[jax.ShapeDtypeStruct((capacity, rows, width), own.dtype)] * count,
        in_specs=[pl.BlockSpec(memory_space=pltpu.SMEM), vmem],
        out_specs=[vmem] * count,
        cost_estimate=pl.CostEstimate(
            flops=0,
            bytes_accessed=2 * own.size + 2 * count * capacity * rows * width,
            transcendentals=0,
        ),
    )(table, own)


def local_kernel(step_ref, index_ref, *refs):
    sources = list(refs[:7])
    masked_ref, masked_t_ref, inv_ref, inv_t_ref = refs[7:11]
    whitened_ref, total_ref = refs[11:13]
    pieces = list(refs[13:19])
    pieces.insert(3, None)
    pulled_ref, half_ref = refs[19:21]
    own_ref = sources[3]
    near_count = masked_ref.shape[1]
    entries = masked_ref.shape[0] * near_count
    pulled_ref[...] = jnp.zeros(pulled_ref.shape, jnp.float32)

    def pull(entry, carry):
        block = entry // near_count
        slot = entry % near_count
        step = step_ref[entry]
        index = index_ref[entry]
        weights = masked_ref[block, slot]
        for k, source in enumerate(sources):

            @pl.when(step == k)
            def _():
                pulled_ref[block] = pulled_ref[block] + jnp.dot(
                    weights, source[index], preferred_element_type=jnp.float32
                )

        return carry

    lax.fori_loop(0, entries, pull, 0)

    def whiten(block, carry):
        conditioned = (own_ref[block].astype(jnp.float32) - pulled_ref[block]).astype(jnp.bfloat16)
        whitened = jnp.dot(
            inv_ref[block], conditioned, preferred_element_type=jnp.float32
        ).astype(jnp.bfloat16)
        whitened_ref[block] = whitened
        lifted = jnp.dot(inv_t_ref[block], whitened, preferred_element_type=jnp.float32)
        total_ref[block] = lifted
        half_ref[block] = lifted.astype(jnp.bfloat16)
        return carry

    lax.fori_loop(0, masked_ref.shape[0], whiten, 0)

    def give_back(entry, carry):
        block = entry // near_count
        slot = entry % near_count
        step = step_ref[entry]
        index = index_ref[entry]
        returned = (
            -jnp.dot(masked_t_ref[block, slot], half_ref[block], preferred_element_type=jnp.float32)
        ).astype(jnp.bfloat16)
        for k, piece in enumerate(pieces):

            @pl.when(step == k)
            def _():
                if piece is None:
                    total_ref[index] = total_ref[index] + returned.astype(jnp.float32)
                else:
                    piece[index] = returned

        return carry

    lax.fori_loop(0, entries, give_back, 0)


def local_stage(step_table, index_table, sources, masked, masked_t, inv, inv_t):
    own = sources[3]
    blocks, rows, width = own.shape
    piece_shape = sources[0].shape
    entries = masked.shape[0] * masked.shape[1]
    vmem = pl.BlockSpec(memory_space=pltpu.VMEM)
    smem = pl.BlockSpec(memory_space=pltpu.SMEM)
    return pl.pallas_call(
        local_kernel,
        out_shape=[
            jax.ShapeDtypeStruct(own.shape, jnp.bfloat16),
            jax.ShapeDtypeStruct(own.shape, jnp.float32),
        ]
        + [jax.ShapeDtypeStruct(piece_shape, jnp.bfloat16)] * 6,
        in_specs=[smem, smem] + [vmem] * 11,
        out_specs=[vmem] * 8,
        scratch_shapes=[
            pltpu.VMEM(own.shape, jnp.float32),
            pltpu.VMEM(own.shape, jnp.bfloat16),
        ],
        compiler_params=pltpu.CompilerParams(vmem_limit_bytes=56 * 1024 * 1024),
        cost_estimate=pl.CostEstimate(
            flops=2 * rows * rows * width * (2 * entries + 2 * blocks),
            bytes_accessed=2 * (2 * own.size + 12 * sources[0].size) + 8 * own.size,
            transcendentals=0,
        ),
    )(step_table, index_table, *sources, masked, masked_t, inv, inv_t)


def accumulate_kernel(target_ref, lifted_ref, *refs):
    pieces = refs[:6]
    out_ref, total_ref = refs[6:8]
    capacity = pieces[0].shape[0]
    total_ref[...] = lifted_ref[...]
    for k, piece in enumerate(pieces):

        def body(slot, carry, k=k, piece=piece):
            target = target_ref[k * capacity + slot]

            @pl.when(target >= 0)
            def _():
                total_ref[target] = total_ref[target] + piece[slot].astype(jnp.float32)

            return carry

        lax.fori_loop(0, capacity, body, 0)
    out_ref[...] = total_ref[...].astype(out_ref.dtype)


def accumulate(target, total, pieces):
    blocks, rows, width = total.shape
    vmem = pl.BlockSpec(memory_space=pltpu.VMEM)
    return pl.pallas_call(
        accumulate_kernel,
        out_shape=jax.ShapeDtypeStruct(total.shape, jnp.bfloat16),
        in_specs=[pl.BlockSpec(memory_space=pltpu.SMEM), vmem] + [vmem] * 6,
        out_specs=vmem,
        scratch_shapes=[pltpu.VMEM(total.shape, jnp.float32)],
        compiler_params=pltpu.CompilerParams(vmem_limit_bytes=56 * 1024 * 1024),
        cost_estimate=pl.CostEstimate(
            flops=6 * pieces[0].size,
            bytes_accessed=6 * total.size + 12 * pieces[0].size,
            transcendentals=0,
        ),
    )(target, total, *pieces)


def local(field, storm_cov, order, neighbours, coeffs, inv_factors):
    node_rows, storm_cols = field.shape
    per_device, near_count, block_size, _ = coeffs.shape
    devices = lax.axis_size("blk")
    device = lax.axis_index("blk")
    slot_count = near_count * per_device
    span = 2 * REACH + 1
    capacity = (slot_count + span - 1) // span

    field_all = lax.all_gather(field, "st", axis=1, tiled=True)

    listed = neighbours.reshape(devices, slot_count)
    owners = listed // per_device
    local_all = listed - owners * per_device
    earlier = jnp.tril(jnp.ones((slot_count, slot_count), jnp.bool_), -1)
    same_owner = owners[:, :, None] == owners[:, None, :]
    ordinal = jnp.sum(same_owner & earlier[None], axis=2)
    my_owners = lax.dynamic_index_in_dim(owners, device, 0, keepdims=False)
    my_rank = lax.dynamic_index_in_dim(ordinal, device, 0, keepdims=False)
    gap = (device - my_owners + devices) % devices
    step_of = jnp.where(gap <= REACH, gap, gap - devices)
    cap_ids = jnp.arange(capacity, dtype=jnp.int32)
    my_local = lax.dynamic_index_in_dim(local_all, device, 0, keepdims=False)
    step_table = step_of + REACH
    index_table = jnp.where(step_of == 0, my_local, my_rank)
    pickers = []
    targets = []
    for step in range(-REACH, REACH + 1):
        if step == 0:
            continue
        reader = (device + step + devices) % devices
        reader_owners = lax.dynamic_index_in_dim(owners, reader, 0, keepdims=False)
        reader_rank = lax.dynamic_index_in_dim(ordinal, reader, 0, keepdims=False)
        reader_local = lax.dynamic_index_in_dim(local_all, reader, 0, keepdims=False)
        chosen = (reader_owners == device)[None, :] & (reader_rank[None, :] == cap_ids[:, None])
        used = jnp.any(chosen, axis=1)
        picked = jnp.sum(jnp.where(chosen, reader_local[None, :], 0), axis=1)
        pickers.append(picked)
        targets.append(jnp.where(used, picked, -1))
    all_targets = jnp.concatenate(targets, axis=0)
    all_pickers = jnp.concatenate(pickers, axis=0)

    mine_listed = lax.dynamic_slice_in_dim(neighbours, device * per_device, per_device, 0)
    block_ids = jnp.arange(order.shape[0], dtype=jnp.int32)
    nbr_order = jnp.sum(jnp.where(mine_listed[:, :, None] == block_ids, order, 0), axis=2)
    own_order = lax.dynamic_slice_in_dim(order, device * per_device, per_device, 0)
    usable = nbr_order < own_order[:, None]
    masked = jnp.where(usable[:, :, None, None], coeffs, jnp.zeros((), jnp.bfloat16))
    masked_t = jnp.swapaxes(masked, 2, 3)
    inv_t = jnp.swapaxes(inv_factors, 1, 2)

    width = storm_cols // CHUNKS
    whitened_parts = []
    product_parts = []
    for chunk in range(CHUNKS):
        rows = storm_cov[chunk * width : (chunk + 1) * width]
        mixed = lax.dot_general(
            field_all, rows, (((1,), (1,)), ((), ())), preferred_element_type=jnp.float32
        ).astype(jnp.bfloat16)
        own_blocks = mixed.reshape(per_device, block_size, width)
        outgoing = pick(all_pickers, own_blocks, capacity, 2 * REACH)
        sources = []
        for k, step in enumerate([s for s in range(-REACH, REACH + 1) if s != 0]):
            sources.append(from_behind(outgoing[k], "blk", step))
        sources.insert(REACH, own_blocks)
        outs = local_stage(step_table, index_table, sources, masked, masked_t, inv_factors, inv_t)
        whitened, total = outs[0], outs[1]
        backs = []
        for k, step in enumerate([s for s in range(-REACH, REACH + 1) if s != 0]):
            backs.append(from_behind(outs[2 + k], "blk", -step))
        product = accumulate(all_targets, total, backs)
        whitened_parts.append(whitened.reshape(node_rows, width))
        product_parts.append(product.reshape(node_rows, width))
    if CHUNKS == 1:
        return whitened_parts[0], product_parts[0]
    return jnp.concatenate(whitened_parts, axis=1), jnp.concatenate(product_parts, axis=1)


def solution(mesh):
    in_specs = (
        P("blk", "st"),
        P("st", None),
        P(),
        P(),
        P("blk", None, None, None),
        P("blk", None, None),
    )
    out_specs = (P("blk", "st"), P("blk", "st"))
    return jax.shard_map(local, mesh=mesh, in_specs=in_specs, out_specs=out_specs, check_vma=False)
```

```python
import jax
import jax.numpy as jnp
from jax import lax
from jax.experimental import pallas as pl
from jax.experimental.pallas import tpu as pltpu
from jax.sharding import PartitionSpec as P

REACH = 3
CHUNKS = 2


def from_behind(array, axis, by):
    count = lax.axis_size(axis)
    return lax.ppermute(array, axis, [(i, (i + by) % count) for i in range(count)])


def pick_kernel(table_ref, own_ref, *pieces):
    capacity = pieces[0].shape[0]
    for k, piece in enumerate(pieces):

        def body(slot, carry, k=k, piece=piece):
            piece[slot] = own_ref[table_ref[k * capacity + slot]]
            return carry

        lax.fori_loop(0, capacity, body, 0)


def pick(table, own, capacity, count):
    blocks, rows, width = own.shape
    vmem = pl.BlockSpec(memory_space=pltpu.VMEM)
    return pl.pallas_call(
        pick_kernel,
        out_shape=[jax.ShapeDtypeStruct((capacity, rows, width), own.dtype)] * count,
        in_specs=[pl.BlockSpec(memory_space=pltpu.SMEM), vmem],
        out_specs=[vmem] * count,
        cost_estimate=pl.CostEstimate(
            flops=0,
            bytes_accessed=2 * own.size + 2 * count * capacity * rows * width,
            transcendentals=0,
        ),
    )(table, own)


def local_kernel(step_ref, index_ref, *refs):
    sources = list(refs[:7])
    wide_ref, wide_t_ref, inv_ref, inv_t_ref = refs[7:11]
    whitened_ref, total_ref = refs[11:13]
    pieces = list(refs[13:19])
    pieces.insert(3, None)
    near_ref, half_ref, returned_ref = refs[19:22]
    own_ref = sources[3]
    blocks, rows, _ = own_ref.shape
    near_count = wide_ref.shape[2] // rows

    def condition(block, carry):
        for slot in range(near_count):
            entry = block * near_count + slot
            step = step_ref[entry]
            index = index_ref[entry]
            for k, source in enumerate(sources):

                @pl.when(step == k)
                def _():
                    near_ref[slot * rows : (slot + 1) * rows] = source[index]

        pulled = jnp.dot(wide_ref[block], near_ref[...], preferred_element_type=jnp.float32)
        conditioned = (own_ref[block].astype(jnp.float32) - pulled).astype(jnp.bfloat16)
        whitened = jnp.dot(
            inv_ref[block], conditioned, preferred_element_type=jnp.float32
        ).astype(jnp.bfloat16)
        whitened_ref[block] = whitened
        lifted = jnp.dot(inv_t_ref[block], whitened, preferred_element_type=jnp.float32)
        total_ref[block] = lifted
        half_ref[block] = lifted.astype(jnp.bfloat16)
        return carry

    lax.fori_loop(0, blocks, condition, 0)

    def give_back(block, carry):
        returned_ref[...] = (
            -jnp.dot(wide_t_ref[block], half_ref[block], preferred_element_type=jnp.float32)
        ).astype(jnp.bfloat16)
        for slot in range(near_count):
            entry = block * near_count + slot
            step = step_ref[entry]
            index = index_ref[entry]
            for k, piece in enumerate(pieces):

                @pl.when(step == k)
                def _():
                    part = returned_ref[slot * rows : (slot + 1) * rows]
                    if piece is None:
                        total_ref[index] = total_ref[index] + part.astype(jnp.float32)
                    else:
                        piece[index] = part

        return carry

    lax.fori_loop(0, blocks, give_back, 0)


def local_stage(step_table, index_table, sources, masked, masked_t, inv, inv_t):
    own = sources[3]
    blocks, rows, width = own.shape
    piece_shape = sources[0].shape
    entries = masked.shape[0] * masked.shape[2] // rows
    vmem = pl.BlockSpec(memory_space=pltpu.VMEM)
    smem = pl.BlockSpec(memory_space=pltpu.SMEM)
    return pl.pallas_call(
        local_kernel,
        out_shape=[
            jax.ShapeDtypeStruct(own.shape, jnp.bfloat16),
            jax.ShapeDtypeStruct(own.shape, jnp.float32),
        ]
        + [jax.ShapeDtypeStruct(piece_shape, jnp.bfloat16)] * 6,
        in_specs=[smem, smem] + [vmem] * 11,
        out_specs=[vmem] * 8,
        scratch_shapes=[
            pltpu.VMEM((masked.shape[2], width), jnp.bfloat16),
            pltpu.VMEM(own.shape, jnp.bfloat16),
            pltpu.VMEM((masked.shape[2], width), jnp.bfloat16),
        ],
        compiler_params=pltpu.CompilerParams(vmem_limit_bytes=56 * 1024 * 1024),
        cost_estimate=pl.CostEstimate(
            flops=2 * rows * rows * width * (2 * entries + 2 * blocks),
            bytes_accessed=2 * (2 * own.size + 12 * sources[0].size) + 8 * own.size,
            transcendentals=0,
        ),
    )(step_table, index_table, *sources, masked, masked_t, inv, inv_t)


def accumulate_kernel(target_ref, lifted_ref, *refs):
    pieces = refs[:6]
    out_ref, total_ref = refs[6:8]
    capacity = pieces[0].shape[0]
    total_ref[...] = lifted_ref[...]
    for k, piece in enumerate(pieces):

        def body(slot, carry, k=k, piece=piece):
            target = target_ref[k * capacity + slot]

            @pl.when(target >= 0)
            def _():
                total_ref[target] = total_ref[target] + piece[slot].astype(jnp.float32)

            return carry

        lax.fori_loop(0, capacity, body, 0)
    out_ref[...] = total_ref[...].astype(out_ref.dtype)


def accumulate(target, total, pieces):
    blocks, rows, width = total.shape
    vmem = pl.BlockSpec(memory_space=pltpu.VMEM)
    return pl.pallas_call(
        accumulate_kernel,
        out_shape=jax.ShapeDtypeStruct(total.shape, jnp.bfloat16),
        in_specs=[pl.BlockSpec(memory_space=pltpu.SMEM), vmem] + [vmem] * 6,
        out_specs=vmem,
        scratch_shapes=[pltpu.VMEM(total.shape, jnp.float32)],
        compiler_params=pltpu.CompilerParams(vmem_limit_bytes=56 * 1024 * 1024),
        cost_estimate=pl.CostEstimate(
            flops=6 * pieces[0].size,
            bytes_accessed=6 * total.size + 12 * pieces[0].size,
            transcendentals=0,
        ),
    )(target, total, *pieces)


def local(field, storm_cov, order, neighbours, coeffs, inv_factors):
    node_rows, storm_cols = field.shape
    per_device, near_count, block_size, _ = coeffs.shape
    devices = lax.axis_size("blk")
    device = lax.axis_index("blk")
    slot_count = near_count * per_device
    span = 2 * REACH + 1
    capacity = (slot_count + span - 1) // span

    field_all = lax.all_gather(field, "st", axis=1, tiled=True)

    listed = neighbours.reshape(devices, slot_count)
    owners = listed // per_device
    local_all = listed - owners * per_device
    earlier = jnp.tril(jnp.ones((slot_count, slot_count), jnp.bool_), -1)
    same_owner = owners[:, :, None] == owners[:, None, :]
    ordinal = jnp.sum(same_owner & earlier[None], axis=2)
    my_owners = lax.dynamic_index_in_dim(owners, device, 0, keepdims=False)
    my_rank = lax.dynamic_index_in_dim(ordinal, device, 0, keepdims=False)
    gap = (device - my_owners + devices) % devices
    step_of = jnp.where(gap <= REACH, gap, gap - devices)
    cap_ids = jnp.arange(capacity, dtype=jnp.int32)
    my_local = lax.dynamic_index_in_dim(local_all, device, 0, keepdims=False)
    step_table = step_of + REACH
    index_table = jnp.where(step_of == 0, my_local, my_rank)
    pickers = []
    targets = []
    for step in range(-REACH, REACH + 1):
        if step == 0:
            continue
        reader = (device + step + devices) % devices
        reader_owners = lax.dynamic_index_in_dim(owners, reader, 0, keepdims=False)
        reader_rank = lax.dynamic_index_in_dim(ordinal, reader, 0, keepdims=False)
        reader_local = lax.dynamic_index_in_dim(local_all, reader, 0, keepdims=False)
        chosen = (reader_owners == device)[None, :] & (reader_rank[None, :] == cap_ids[:, None])
        used = jnp.any(chosen, axis=1)
        picked = jnp.sum(jnp.where(chosen, reader_local[None, :], 0), axis=1)
        pickers.append(picked)
        targets.append(jnp.where(used, picked, -1))
    all_targets = jnp.concatenate(targets, axis=0)
    all_pickers = jnp.concatenate(pickers, axis=0)

    mine_listed = lax.dynamic_slice_in_dim(neighbours, device * per_device, per_device, 0)
    block_ids = jnp.arange(order.shape[0], dtype=jnp.int32)
    nbr_order = jnp.sum(jnp.where(mine_listed[:, :, None] == block_ids, order, 0), axis=2)
    own_order = lax.dynamic_slice_in_dim(order, device * per_device, per_device, 0)
    usable = nbr_order < own_order[:, None]
    masked = jnp.where(usable[:, :, None, None], coeffs, jnp.zeros((), jnp.bfloat16))
    wide = jnp.transpose(masked, (0, 2, 1, 3)).reshape(per_device, block_size, slot_count // per_device * block_size)
    wide_t = jnp.swapaxes(masked, 2, 3).reshape(per_device, slot_count // per_device * block_size, block_size)
    inv_t = jnp.swapaxes(inv_factors, 1, 2)

    width = storm_cols // CHUNKS
    whitened_parts = []
    product_parts = []
    for chunk in range(CHUNKS):
        rows = storm_cov[chunk * width : (chunk + 1) * width]
        mixed = lax.dot_general(
            field_all, rows, (((1,), (1,)), ((), ())), preferred_element_type=jnp.float32
        ).astype(jnp.bfloat16)
        own_blocks = mixed.reshape(per_device, block_size, width)
        outgoing = pick(all_pickers, own_blocks, capacity, 2 * REACH)
        sources = []
        for k, step in enumerate([s for s in range(-REACH, REACH + 1) if s != 0]):
            sources.append(from_behind(outgoing[k], "blk", step))
        sources.insert(REACH, own_blocks)
        outs = local_stage(step_table, index_table, sources, wide, wide_t, inv_factors, inv_t)
        whitened, total = outs[0], outs[1]
        backs = []
        for k, step in enumerate([s for s in range(-REACH, REACH + 1) if s != 0]):
            backs.append(from_behind(outs[2 + k], "blk", -step))
        product = accumulate(all_targets, total, backs)
        whitened_parts.append(whitened.reshape(node_rows, width))
        product_parts.append(product.reshape(node_rows, width))
    if CHUNKS == 1:
        return whitened_parts[0], product_parts[0]
    return jnp.concatenate(whitened_parts, axis=1), jnp.concatenate(product_parts, axis=1)


def solution(mesh):
    in_specs = (
        P("blk", "st"),
        P("st", None),
        P(),
        P(),
        P("blk", None, None, None),
        P("blk", None, None),
    )
    out_specs = (P("blk", "st"), P("blk", "st"))
    return jax.shard_map(local, mesh=mesh, in_specs=in_specs, out_specs=out_specs, check_vma=False)
```

```python
import jax
import jax.numpy as jnp
from jax import lax
from jax.experimental import pallas as pl
from jax.experimental.pallas import tpu as pltpu
from jax.sharding import PartitionSpec as P

REACH = 3
CHUNKS = 2


def from_behind(array, axis, by):
    count = lax.axis_size(axis)
    return lax.ppermute(array, axis, [(i, (i + by) % count) for i in range(count)])


def pick_kernel(table_ref, own_ref, *pieces):
    capacity = pieces[0].shape[0]
    for k, piece in enumerate(pieces):

        def body(slot, carry, k=k, piece=piece):
            piece[slot] = own_ref[table_ref[k * capacity + slot]]
            return carry

        lax.fori_loop(0, capacity, body, 0)


def pick(table, own, capacity, count):
    blocks, rows, width = own.shape
    vmem = pl.BlockSpec(memory_space=pltpu.VMEM)
    return pl.pallas_call(
        pick_kernel,
        out_shape=[jax.ShapeDtypeStruct((capacity, rows, width), own.dtype)] * count,
        in_specs=[pl.BlockSpec(memory_space=pltpu.SMEM), vmem],
        out_specs=[vmem] * count,
        cost_estimate=pl.CostEstimate(
            flops=0,
            bytes_accessed=2 * own.size + 2 * count * capacity * rows * width,
            transcendentals=0,
        ),
    )(table, own)


def local_kernel(bounds_ref, entry_ref, index_ref, *refs):
    sources = list(refs[:7])
    wide_ref, wide_t_ref, inv_ref, inv_t_ref = refs[7:11]
    whitened_ref, total_ref = refs[11:13]
    pieces = list(refs[13:19])
    pieces.insert(3, None)
    near_ref, half_ref, returned_ref = refs[19:22]
    own_ref = sources[3]
    blocks, rows, _ = own_ref.shape
    span = wide_ref.shape[2]

    for k, source in enumerate(sources):

        def fetch(position, carry, source=source):
            entry = entry_ref[position]
            start = pl.multiple_of(entry * rows, rows)
            near_ref[pl.ds(start, rows)] = source[index_ref[entry]]
            return carry

        lax.fori_loop(bounds_ref[k], bounds_ref[k + 1], fetch, 0)

    def condition(block, carry):
        start = pl.multiple_of(block * span, span)
        pulled = jnp.dot(
            wide_ref[block], near_ref[pl.ds(start, span)], preferred_element_type=jnp.float32
        )
        conditioned = (own_ref[block].astype(jnp.float32) - pulled).astype(jnp.bfloat16)
        whitened = jnp.dot(
            inv_ref[block], conditioned, preferred_element_type=jnp.float32
        ).astype(jnp.bfloat16)
        whitened_ref[block] = whitened
        lifted = jnp.dot(inv_t_ref[block], whitened, preferred_element_type=jnp.float32)
        total_ref[block] = lifted
        half_ref[block] = lifted.astype(jnp.bfloat16)
        return carry

    lax.fori_loop(0, blocks, condition, 0)

    def give_back(block, carry):
        start = pl.multiple_of(block * span, span)
        returned_ref[pl.ds(start, span)] = (
            -jnp.dot(wide_t_ref[block], half_ref[block], preferred_element_type=jnp.float32)
        ).astype(jnp.bfloat16)
        return carry

    lax.fori_loop(0, blocks, give_back, 0)

    for k, piece in enumerate(pieces):

        def store(position, carry, piece=piece):
            entry = entry_ref[position]
            index = index_ref[entry]
            start = pl.multiple_of(entry * rows, rows)
            part = returned_ref[pl.ds(start, rows)]
            if piece is None:
                total_ref[index] = total_ref[index] + part.astype(jnp.float32)
            else:
                piece[index] = part
            return carry

        lax.fori_loop(bounds_ref[k], bounds_ref[k + 1], store, 0)


def local_stage(bounds, entry_order, index_table, sources, masked, masked_t, inv, inv_t):
    own = sources[3]
    blocks, rows, width = own.shape
    piece_shape = sources[0].shape
    entries = masked.shape[0] * masked.shape[2] // rows
    vmem = pl.BlockSpec(memory_space=pltpu.VMEM)
    smem = pl.BlockSpec(memory_space=pltpu.SMEM)
    return pl.pallas_call(
        local_kernel,
        out_shape=[
            jax.ShapeDtypeStruct(own.shape, jnp.bfloat16),
            jax.ShapeDtypeStruct(own.shape, jnp.float32),
        ]
        + [jax.ShapeDtypeStruct(piece_shape, jnp.bfloat16)] * 6,
        in_specs=[smem, smem, smem] + [vmem] * 11,
        out_specs=[vmem] * 8,
        scratch_shapes=[
            pltpu.VMEM((entries * rows, width), jnp.bfloat16),
            pltpu.VMEM(own.shape, jnp.bfloat16),
            pltpu.VMEM((entries * rows, width), jnp.bfloat16),
        ],
        compiler_params=pltpu.CompilerParams(vmem_limit_bytes=56 * 1024 * 1024),
        cost_estimate=pl.CostEstimate(
            flops=2 * rows * rows * width * (2 * entries + 2 * blocks),
            bytes_accessed=2 * (2 * own.size + 12 * sources[0].size) + 8 * own.size,
            transcendentals=0,
        ),
    )(bounds, entry_order, index_table, *sources, masked, masked_t, inv, inv_t)


def accumulate_kernel(target_ref, lifted_ref, *refs):
    pieces = refs[:6]
    out_ref, total_ref = refs[6:8]
    capacity = pieces[0].shape[0]
    total_ref[...] = lifted_ref[...]
    for k, piece in enumerate(pieces):

        def body(slot, carry, k=k, piece=piece):
            target = target_ref[k * capacity + slot]

            @pl.when(target >= 0)
            def _():
                total_ref[target] = total_ref[target] + piece[slot].astype(jnp.float32)

            return carry

        lax.fori_loop(0, capacity, body, 0)
    out_ref[...] = total_ref[...].astype(out_ref.dtype)


def accumulate(target, total, pieces):
    blocks, rows, width = total.shape
    vmem = pl.BlockSpec(memory_space=pltpu.VMEM)
    return pl.pallas_call(
        accumulate_kernel,
        out_shape=jax.ShapeDtypeStruct(total.shape, jnp.bfloat16),
        in_specs=[pl.BlockSpec(memory_space=pltpu.SMEM), vmem] + [vmem] * 6,
        out_specs=vmem,
        scratch_shapes=[pltpu.VMEM(total.shape, jnp.float32)],
        compiler_params=pltpu.CompilerParams(vmem_limit_bytes=56 * 1024 * 1024),
        cost_estimate=pl.CostEstimate(
            flops=6 * pieces[0].size,
            bytes_accessed=6 * total.size + 12 * pieces[0].size,
            transcendentals=0,
        ),
    )(target, total, *pieces)


def local(field, storm_cov, order, neighbours, coeffs, inv_factors):
    node_rows, storm_cols = field.shape
    per_device, near_count, block_size, _ = coeffs.shape
    devices = lax.axis_size("blk")
    device = lax.axis_index("blk")
    slot_count = near_count * per_device
    span = 2 * REACH + 1
    capacity = (slot_count + span - 1) // span

    field_all = lax.all_gather(field, "st", axis=1, tiled=True)

    listed = neighbours.reshape(devices, slot_count)
    owners = listed // per_device
    local_all = listed - owners * per_device
    earlier = jnp.tril(jnp.ones((slot_count, slot_count), jnp.bool_), -1)
    same_owner = owners[:, :, None] == owners[:, None, :]
    ordinal = jnp.sum(same_owner & earlier[None], axis=2)
    my_owners = lax.dynamic_index_in_dim(owners, device, 0, keepdims=False)
    my_rank = lax.dynamic_index_in_dim(ordinal, device, 0, keepdims=False)
    gap = (device - my_owners + devices) % devices
    step_of = jnp.where(gap <= REACH, gap, gap - devices)
    cap_ids = jnp.arange(capacity, dtype=jnp.int32)
    my_local = lax.dynamic_index_in_dim(local_all, device, 0, keepdims=False)
    step_table = step_of + REACH
    index_table = jnp.where(step_of == 0, my_local, my_rank)
    step_ids = jnp.arange(span, dtype=jnp.int32)
    per_step = jnp.sum(step_table[None, :] == step_ids[:, None], axis=1)
    bounds = jnp.concatenate([jnp.zeros((1,), jnp.int32), jnp.cumsum(per_step)]).astype(jnp.int32)
    entry_ids = jnp.arange(slot_count, dtype=jnp.int32)
    same_before = jnp.sum(
        (step_table[None, :] == step_table[:, None]) & (entry_ids[None, :] < entry_ids[:, None]),
        axis=1,
    )
    position = bounds[step_table] + same_before
    entry_order = jnp.sum(
        jnp.where(position[None, :] == entry_ids[:, None], entry_ids[None, :], 0), axis=1
    ).astype(jnp.int32)
    pickers = []
    targets = []
    for step in range(-REACH, REACH + 1):
        if step == 0:
            continue
        reader = (device + step + devices) % devices
        reader_owners = lax.dynamic_index_in_dim(owners, reader, 0, keepdims=False)
        reader_rank = lax.dynamic_index_in_dim(ordinal, reader, 0, keepdims=False)
        reader_local = lax.dynamic_index_in_dim(local_all, reader, 0, keepdims=False)
        chosen = (reader_owners == device)[None, :] & (reader_rank[None, :] == cap_ids[:, None])
        used = jnp.any(chosen, axis=1)
        picked = jnp.sum(jnp.where(chosen, reader_local[None, :], 0), axis=1)
        pickers.append(picked)
        targets.append(jnp.where(used, picked, -1))
    all_targets = jnp.concatenate(targets, axis=0)
    all_pickers = jnp.concatenate(pickers, axis=0)

    mine_listed = lax.dynamic_slice_in_dim(neighbours, device * per_device, per_device, 0)
    block_ids = jnp.arange(order.shape[0], dtype=jnp.int32)
    nbr_order = jnp.sum(jnp.where(mine_listed[:, :, None] == block_ids, order, 0), axis=2)
    own_order = lax.dynamic_slice_in_dim(order, device * per_device, per_device, 0)
    usable = nbr_order < own_order[:, None]
    masked = jnp.where(usable[:, :, None, None], coeffs, jnp.zeros((), jnp.bfloat16))
    wide = jnp.transpose(masked, (0, 2, 1, 3)).reshape(per_device, block_size, slot_count // per_device * block_size)
    wide_t = jnp.swapaxes(masked, 2, 3).reshape(per_device, slot_count // per_device * block_size, block_size)
    inv_t = jnp.swapaxes(inv_factors, 1, 2)

    width = storm_cols // CHUNKS
    whitened_parts = []
    product_parts = []
    for chunk in range(CHUNKS):
        rows = storm_cov[chunk * width : (chunk + 1) * width]
        mixed = lax.dot_general(
            field_all, rows, (((1,), (1,)), ((), ())), preferred_element_type=jnp.float32
        ).astype(jnp.bfloat16)
        own_blocks = mixed.reshape(per_device, block_size, width)
        outgoing = pick(all_pickers, own_blocks, capacity, 2 * REACH)
        sources = []
        for k, step in enumerate([s for s in range(-REACH, REACH + 1) if s != 0]):
            sources.append(from_behind(outgoing[k], "blk", step))
        sources.insert(REACH, own_blocks)
        outs = local_stage(
            bounds, entry_order, index_table, sources, wide, wide_t, inv_factors, inv_t
        )
        whitened, total = outs[0], outs[1]
        backs = []
        for k, step in enumerate([s for s in range(-REACH, REACH + 1) if s != 0]):
            backs.append(from_behind(outs[2 + k], "blk", -step))
        product = accumulate(all_targets, total, backs)
        whitened_parts.append(whitened.reshape(node_rows, width))
        product_parts.append(product.reshape(node_rows, width))
    if CHUNKS == 1:
        return whitened_parts[0], product_parts[0]
    return jnp.concatenate(whitened_parts, axis=1), jnp.concatenate(product_parts, axis=1)


def solution(mesh):
    in_specs = (
        P("blk", "st"),
        P("st", None),
        P(),
        P(),
        P("blk", None, None, None),
        P("blk", None, None),
    )
    out_specs = (P("blk", "st"), P("blk", "st"))
    return jax.shard_map(local, mesh=mesh, in_specs=in_specs, out_specs=out_specs, check_vma=False)
```

```python
import jax
import jax.numpy as jnp
from jax import lax
from jax.experimental import pallas as pl
from jax.experimental.pallas import tpu as pltpu
from jax.sharding import PartitionSpec as P

REACH = 3
CHUNKS = 2


def from_behind(array, axis, by):
    count = lax.axis_size(axis)
    return lax.ppermute(array, axis, [(i, (i + by) % count) for i in range(count)])


def pick_kernel(table_ref, own_ref, *pieces):
    capacity = pieces[0].shape[0]
    for k, piece in enumerate(pieces):

        def body(slot, carry, k=k, piece=piece):
            piece[slot] = own_ref[table_ref[k * capacity + slot]]
            return carry

        lax.fori_loop(0, capacity, body, 0)


def pick(table, own, capacity, count):
    blocks, rows, width = own.shape
    vmem = pl.BlockSpec(memory_space=pltpu.VMEM)
    return pl.pallas_call(
        pick_kernel,
        out_shape=[jax.ShapeDtypeStruct((capacity, rows, width), own.dtype)] * count,
        in_specs=[pl.BlockSpec(memory_space=pltpu.SMEM), vmem],
        out_specs=[vmem] * count,
        cost_estimate=pl.CostEstimate(
            flops=0,
            bytes_accessed=2 * own.size + 2 * count * capacity * rows * width,
            transcendentals=0,
        ),
    )(table, own)


def local_kernel(bounds_ref, entry_ref, index_ref, *refs):
    sources = list(refs[:7])
    wide_ref, wide_t_ref, inv_ref, inv_t_ref = refs[7:11]
    whitened_ref, total_ref = refs[11:13]
    pieces = list(refs[13:19])
    pieces.insert(3, None)
    near_ref, half_ref, returned_ref = refs[19:22]
    own_ref = sources[3]
    blocks, rows, _ = own_ref.shape
    span = wide_ref.shape[2]

    for k, source in enumerate(sources):

        def fetch(position, carry, source=source):
            entry = entry_ref[position]
            start = pl.multiple_of(entry * rows, rows)
            near_ref[pl.ds(start, rows)] = source[index_ref[entry]]
            return carry

        lax.fori_loop(bounds_ref[k], bounds_ref[k + 1], fetch, 0)

    def condition(block, carry):
        start = pl.multiple_of(block * span, span)
        pulled = jnp.dot(
            wide_ref[block], near_ref[pl.ds(start, span)], preferred_element_type=jnp.float32
        )
        conditioned = (own_ref[block].astype(jnp.float32) - pulled).astype(jnp.bfloat16)
        whitened = jnp.dot(
            inv_ref[block], conditioned, preferred_element_type=jnp.float32
        ).astype(jnp.bfloat16)
        whitened_ref[block] = whitened
        lifted = jnp.dot(inv_t_ref[block], whitened, preferred_element_type=jnp.float32)
        total_ref[block] = lifted
        half_ref[block] = lifted.astype(jnp.bfloat16)
        return carry

    lax.fori_loop(0, blocks, condition, 0)

    def give_back(block, carry):
        start = pl.multiple_of(block * span, span)
        returned_ref[pl.ds(start, span)] = (
            -jnp.dot(wide_t_ref[block], half_ref[block], preferred_element_type=jnp.float32)
        ).astype(jnp.bfloat16)
        return carry

    lax.fori_loop(0, blocks, give_back, 0)

    for k, piece in enumerate(pieces):

        def store(position, carry, piece=piece):
            entry = entry_ref[position]
            index = index_ref[entry]
            start = pl.multiple_of(entry * rows, rows)
            part = returned_ref[pl.ds(start, rows)]
            if piece is None:
                total_ref[index] = total_ref[index] + part.astype(jnp.float32)
            else:
                piece[index] = part
            return carry

        lax.fori_loop(bounds_ref[k], bounds_ref[k + 1], store, 0)


def local_stage(bounds, entry_order, index_table, sources, masked, masked_t, inv, inv_t):
    own = sources[3]
    blocks, rows, width = own.shape
    piece_shape = sources[0].shape
    entries = masked.shape[0] * masked.shape[2] // rows
    vmem = pl.BlockSpec(memory_space=pltpu.VMEM)
    smem = pl.BlockSpec(memory_space=pltpu.SMEM)
    return pl.pallas_call(
        local_kernel,
        out_shape=[
            jax.ShapeDtypeStruct(own.shape, jnp.bfloat16),
            jax.ShapeDtypeStruct(own.shape, jnp.float32),
        ]
        + [jax.ShapeDtypeStruct(piece_shape, jnp.bfloat16)] * 6,
        in_specs=[smem, smem, smem] + [vmem] * 11,
        out_specs=[vmem] * 8,
        scratch_shapes=[
            pltpu.VMEM((entries * rows, width), jnp.bfloat16),
            pltpu.VMEM(own.shape, jnp.bfloat16),
            pltpu.VMEM((entries * rows, width), jnp.bfloat16),
        ],
        compiler_params=pltpu.CompilerParams(vmem_limit_bytes=56 * 1024 * 1024),
        cost_estimate=pl.CostEstimate(
            flops=2 * rows * rows * width * (2 * entries + 2 * blocks),
            bytes_accessed=2 * (2 * own.size + 12 * sources[0].size) + 8 * own.size,
            transcendentals=0,
        ),
    )(bounds, entry_order, index_table, *sources, masked, masked_t, inv, inv_t)


def accumulate_kernel(target_ref, lifted_ref, *refs):
    pieces = refs[:6]
    out_ref, total_ref = refs[6:8]
    capacity = pieces[0].shape[0]
    total_ref[...] = lifted_ref[...]
    for k, piece in enumerate(pieces):

        def body(slot, carry, k=k, piece=piece):
            target = target_ref[k * capacity + slot]

            @pl.when(target >= 0)
            def _():
                total_ref[target] = total_ref[target] + piece[slot].astype(jnp.float32)

            return carry

        lax.fori_loop(0, capacity, body, 0)
    out_ref[...] = total_ref[...].astype(out_ref.dtype)


def accumulate(target, total, pieces):
    blocks, rows, width = total.shape
    vmem = pl.BlockSpec(memory_space=pltpu.VMEM)
    return pl.pallas_call(
        accumulate_kernel,
        out_shape=jax.ShapeDtypeStruct(total.shape, jnp.bfloat16),
        in_specs=[pl.BlockSpec(memory_space=pltpu.SMEM), vmem] + [vmem] * 6,
        out_specs=vmem,
        scratch_shapes=[pltpu.VMEM(total.shape, jnp.float32)],
        compiler_params=pltpu.CompilerParams(vmem_limit_bytes=56 * 1024 * 1024),
        cost_estimate=pl.CostEstimate(
            flops=6 * pieces[0].size,
            bytes_accessed=6 * total.size + 12 * pieces[0].size,
            transcendentals=0,
        ),
    )(target, total, *pieces)


def local(field, storm_cov, order, neighbours, coeffs, inv_factors):
    node_rows, storm_cols = field.shape
    per_device, near_count, block_size, _ = coeffs.shape
    devices = lax.axis_size("blk")
    device = lax.axis_index("blk")
    slot_count = near_count * per_device
    span = 2 * REACH + 1
    capacity = (slot_count + span - 1) // span

    parts = lax.axis_size("st")
    part = lax.axis_index("st")
    if parts == 4:
        half = node_rows // 2
        from_left = from_behind(field, "st", 1)
        from_right = from_behind(field, "st", -1)
        far_top = from_behind(from_right[:half], "st", -1)
        far_bottom = from_behind(from_left[half:], "st", 1)
        shards = [
            (part, field),
            ((part + parts - 1) % parts, from_left),
            ((part + 1) % parts, from_right),
            ((part + 2) % parts, jnp.concatenate([far_top, far_bottom], axis=0)),
        ]
    else:
        field_all = lax.all_gather(field, "st", axis=1, tiled=True)
        shards = [(0, field_all)]

    listed = neighbours.reshape(devices, slot_count)
    owners = listed // per_device
    local_all = listed - owners * per_device
    earlier = jnp.tril(jnp.ones((slot_count, slot_count), jnp.bool_), -1)
    same_owner = owners[:, :, None] == owners[:, None, :]
    ordinal = jnp.sum(same_owner & earlier[None], axis=2)
    my_owners = lax.dynamic_index_in_dim(owners, device, 0, keepdims=False)
    my_rank = lax.dynamic_index_in_dim(ordinal, device, 0, keepdims=False)
    gap = (device - my_owners + devices) % devices
    step_of = jnp.where(gap <= REACH, gap, gap - devices)
    cap_ids = jnp.arange(capacity, dtype=jnp.int32)
    my_local = lax.dynamic_index_in_dim(local_all, device, 0, keepdims=False)
    step_table = step_of + REACH
    index_table = jnp.where(step_of == 0, my_local, my_rank)
    step_ids = jnp.arange(span, dtype=jnp.int32)
    per_step = jnp.sum(step_table[None, :] == step_ids[:, None], axis=1)
    bounds = jnp.concatenate([jnp.zeros((1,), jnp.int32), jnp.cumsum(per_step)]).astype(jnp.int32)
    entry_ids = jnp.arange(slot_count, dtype=jnp.int32)
    same_before = jnp.sum(
        (step_table[None, :] == step_table[:, None]) & (entry_ids[None, :] < entry_ids[:, None]),
        axis=1,
    )
    position = bounds[step_table] + same_before
    entry_order = jnp.sum(
        jnp.where(position[None, :] == entry_ids[:, None], entry_ids[None, :], 0), axis=1
    ).astype(jnp.int32)
    pickers = []
    targets = []
    for step in range(-REACH, REACH + 1):
        if step == 0:
            continue
        reader = (device + step + devices) % devices
        reader_owners = lax.dynamic_index_in_dim(owners, reader, 0, keepdims=False)
        reader_rank = lax.dynamic_index_in_dim(ordinal, reader, 0, keepdims=False)
        reader_local = lax.dynamic_index_in_dim(local_all, reader, 0, keepdims=False)
        chosen = (reader_owners == device)[None, :] & (reader_rank[None, :] == cap_ids[:, None])
        used = jnp.any(chosen, axis=1)
        picked = jnp.sum(jnp.where(chosen, reader_local[None, :], 0), axis=1)
        pickers.append(picked)
        targets.append(jnp.where(used, picked, -1))
    all_targets = jnp.concatenate(targets, axis=0)
    all_pickers = jnp.concatenate(pickers, axis=0)

    mine_listed = lax.dynamic_slice_in_dim(neighbours, device * per_device, per_device, 0)
    block_ids = jnp.arange(order.shape[0], dtype=jnp.int32)
    nbr_order = jnp.sum(jnp.where(mine_listed[:, :, None] == block_ids, order, 0), axis=2)
    own_order = lax.dynamic_slice_in_dim(order, device * per_device, per_device, 0)
    usable = nbr_order < own_order[:, None]
    masked = jnp.where(usable[:, :, None, None], coeffs, jnp.zeros((), jnp.bfloat16))
    wide = jnp.transpose(masked, (0, 2, 1, 3)).reshape(per_device, block_size, slot_count // per_device * block_size)
    wide_t = jnp.swapaxes(masked, 2, 3).reshape(per_device, slot_count // per_device * block_size, block_size)
    inv_t = jnp.swapaxes(inv_factors, 1, 2)

    width = storm_cols // CHUNKS
    whitened_parts = []
    product_parts = []
    for chunk in range(CHUNKS):
        rows = storm_cov[chunk * width : (chunk + 1) * width]
        mixed = None
        for owner, shard in shards:
            cov_part = lax.dynamic_slice_in_dim(
                rows, owner * shard.shape[1], shard.shape[1], axis=1
            )
            term = lax.dot_general(
                shard, cov_part, (((1,), (1,)), ((), ())), preferred_element_type=jnp.float32
            )
            mixed = term if mixed is None else mixed + term
        mixed = mixed.astype(jnp.bfloat16)
        own_blocks = mixed.reshape(per_device, block_size, width)
        outgoing = pick(all_pickers, own_blocks, capacity, 2 * REACH)
        sources = []
        for k, step in enumerate([s for s in range(-REACH, REACH + 1) if s != 0]):
            sources.append(from_behind(outgoing[k], "blk", step))
        sources.insert(REACH, own_blocks)
        outs = local_stage(
            bounds, entry_order, index_table, sources, wide, wide_t, inv_factors, inv_t
        )
        whitened, total = outs[0], outs[1]
        backs = []
        for k, step in enumerate([s for s in range(-REACH, REACH + 1) if s != 0]):
            backs.append(from_behind(outs[2 + k], "blk", -step))
        product = accumulate(all_targets, total, backs)
        whitened_parts.append(whitened.reshape(node_rows, width))
        product_parts.append(product.reshape(node_rows, width))
    if CHUNKS == 1:
        return whitened_parts[0], product_parts[0]
    return jnp.concatenate(whitened_parts, axis=1), jnp.concatenate(product_parts, axis=1)


def solution(mesh):
    in_specs = (
        P("blk", "st"),
        P("st", None),
        P(),
        P(),
        P("blk", None, None, None),
        P("blk", None, None),
    )
    out_specs = (P("blk", "st"), P("blk", "st"))
    return jax.shard_map(local, mesh=mesh, in_specs=in_specs, out_specs=out_specs, check_vma=False)
```

```python
import jax
import jax.numpy as jnp
from jax import lax
from jax.experimental import pallas as pl
from jax.experimental.pallas import tpu as pltpu
from jax.sharding import PartitionSpec as P

REACH = 3
CHUNKS = 4


def from_behind(array, axis, by):
    count = lax.axis_size(axis)
    return lax.ppermute(array, axis, [(i, (i + by) % count) for i in range(count)])


def pick_kernel(table_ref, own_ref, *pieces):
    capacity = pieces[0].shape[0]
    for k, piece in enumerate(pieces):

        def body(slot, carry, k=k, piece=piece):
            piece[slot] = own_ref[table_ref[k * capacity + slot]]
            return carry

        lax.fori_loop(0, capacity, body, 0)


def pick(table, own, capacity, count):
    blocks, rows, width = own.shape
    vmem = pl.BlockSpec(memory_space=pltpu.VMEM)
    return pl.pallas_call(
        pick_kernel,
        out_shape=[jax.ShapeDtypeStruct((capacity, rows, width), own.dtype)] * count,
        in_specs=[pl.BlockSpec(memory_space=pltpu.SMEM), vmem],
        out_specs=[vmem] * count,
        cost_estimate=pl.CostEstimate(
            flops=0,
            bytes_accessed=2 * own.size + 2 * count * capacity * rows * width,
            transcendentals=0,
        ),
    )(table, own)


def local_kernel(bounds_ref, entry_ref, index_ref, *refs):
    sources = list(refs[:7])
    wide_ref, wide_t_ref, inv_ref, inv_t_ref = refs[7:11]
    whitened_ref, total_ref = refs[11:13]
    pieces = list(refs[13:19])
    pieces.insert(3, None)
    near_ref, half_ref, returned_ref = refs[19:22]
    own_ref = sources[3]
    blocks, rows, _ = own_ref.shape
    span = wide_ref.shape[2]

    for k, source in enumerate(sources):

        def fetch(position, carry, source=source):
            entry = entry_ref[position]
            start = pl.multiple_of(entry * rows, rows)
            near_ref[pl.ds(start, rows)] = source[index_ref[entry]]
            return carry

        lax.fori_loop(bounds_ref[k], bounds_ref[k + 1], fetch, 0)

    def condition(block, carry):
        start = pl.multiple_of(block * span, span)
        pulled = jnp.dot(
            wide_ref[block], near_ref[pl.ds(start, span)], preferred_element_type=jnp.float32
        )
        conditioned = (own_ref[block].astype(jnp.float32) - pulled).astype(jnp.bfloat16)
        whitened = jnp.dot(
            inv_ref[block], conditioned, preferred_element_type=jnp.float32
        ).astype(jnp.bfloat16)
        whitened_ref[block] = whitened
        lifted = jnp.dot(inv_t_ref[block], whitened, preferred_element_type=jnp.float32)
        total_ref[block] = lifted
        half_ref[block] = lifted.astype(jnp.bfloat16)
        return carry

    lax.fori_loop(0, blocks, condition, 0)

    def give_back(block, carry):
        start = pl.multiple_of(block * span, span)
        returned_ref[pl.ds(start, span)] = (
            -jnp.dot(wide_t_ref[block], half_ref[block], preferred_element_type=jnp.float32)
        ).astype(jnp.bfloat16)
        return carry

    lax.fori_loop(0, blocks, give_back, 0)

    for k, piece in enumerate(pieces):

        def store(position, carry, piece=piece):
            entry = entry_ref[position]
            index = index_ref[entry]
            start = pl.multiple_of(entry * rows, rows)
            part = returned_ref[pl.ds(start, rows)]
            if piece is None:
                total_ref[index] = total_ref[index] + part.astype(jnp.float32)
            else:
                piece[index] = part
            return carry

        lax.fori_loop(bounds_ref[k], bounds_ref[k + 1], store, 0)


def local_stage(bounds, entry_order, index_table, sources, masked, masked_t, inv, inv_t):
    own = sources[3]
    blocks, rows, width = own.shape
    piece_shape = sources[0].shape
    entries = masked.shape[0] * masked.shape[2] // rows
    vmem = pl.BlockSpec(memory_space=pltpu.VMEM)
    smem = pl.BlockSpec(memory_space=pltpu.SMEM)
    return pl.pallas_call(
        local_kernel,
        out_shape=[
            jax.ShapeDtypeStruct(own.shape, jnp.bfloat16),
            jax.ShapeDtypeStruct(own.shape, jnp.float32),
        ]
        + [jax.ShapeDtypeStruct(piece_shape, jnp.bfloat16)] * 6,
        in_specs=[smem, smem, smem] + [vmem] * 11,
        out_specs=[vmem] * 8,
        scratch_shapes=[
            pltpu.VMEM((entries * rows, width), jnp.bfloat16),
            pltpu.VMEM(own.shape, jnp.bfloat16),
            pltpu.VMEM((entries * rows, width), jnp.bfloat16),
        ],
        compiler_params=pltpu.CompilerParams(vmem_limit_bytes=56 * 1024 * 1024),
        cost_estimate=pl.CostEstimate(
            flops=2 * rows * rows * width * (2 * entries + 2 * blocks),
            bytes_accessed=2 * (2 * own.size + 12 * sources[0].size) + 8 * own.size,
            transcendentals=0,
        ),
    )(bounds, entry_order, index_table, *sources, masked, masked_t, inv, inv_t)


def accumulate_kernel(target_ref, lifted_ref, *refs):
    pieces = refs[:6]
    out_ref, total_ref = refs[6:8]
    capacity = pieces[0].shape[0]
    total_ref[...] = lifted_ref[...]
    for k, piece in enumerate(pieces):

        def body(slot, carry, k=k, piece=piece):
            target = target_ref[k * capacity + slot]

            @pl.when(target >= 0)
            def _():
                total_ref[target] = total_ref[target] + piece[slot].astype(jnp.float32)

            return carry

        lax.fori_loop(0, capacity, body, 0)
    out_ref[...] = total_ref[...].astype(out_ref.dtype)


def accumulate(target, total, pieces):
    blocks, rows, width = total.shape
    vmem = pl.BlockSpec(memory_space=pltpu.VMEM)
    return pl.pallas_call(
        accumulate_kernel,
        out_shape=jax.ShapeDtypeStruct(total.shape, jnp.bfloat16),
        in_specs=[pl.BlockSpec(memory_space=pltpu.SMEM), vmem] + [vmem] * 6,
        out_specs=vmem,
        scratch_shapes=[pltpu.VMEM(total.shape, jnp.float32)],
        compiler_params=pltpu.CompilerParams(vmem_limit_bytes=56 * 1024 * 1024),
        cost_estimate=pl.CostEstimate(
            flops=6 * pieces[0].size,
            bytes_accessed=6 * total.size + 12 * pieces[0].size,
            transcendentals=0,
        ),
    )(target, total, *pieces)


def local(field, storm_cov, order, neighbours, coeffs, inv_factors):
    node_rows, storm_cols = field.shape
    per_device, near_count, block_size, _ = coeffs.shape
    devices = lax.axis_size("blk")
    device = lax.axis_index("blk")
    slot_count = near_count * per_device
    span = 2 * REACH + 1
    capacity = (slot_count + span - 1) // span

    parts = lax.axis_size("st")
    part = lax.axis_index("st")
    if parts == 4:
        half = node_rows // 2
        from_left = from_behind(field, "st", 1)
        from_right = from_behind(field, "st", -1)
        far_top = from_behind(from_right[:half], "st", -1)
        far_bottom = from_behind(from_left[half:], "st", 1)
        shards = [
            (part, field),
            ((part + parts - 1) % parts, from_left),
            ((part + 1) % parts, from_right),
            ((part + 2) % parts, jnp.concatenate([far_top, far_bottom], axis=0)),
        ]
    else:
        field_all = lax.all_gather(field, "st", axis=1, tiled=True)
        shards = [(0, field_all)]

    listed = neighbours.reshape(devices, slot_count)
    owners = listed // per_device
    local_all = listed - owners * per_device
    earlier = jnp.tril(jnp.ones((slot_count, slot_count), jnp.bool_), -1)
    same_owner = owners[:, :, None] == owners[:, None, :]
    ordinal = jnp.sum(same_owner & earlier[None], axis=2)
    my_owners = lax.dynamic_index_in_dim(owners, device, 0, keepdims=False)
    my_rank = lax.dynamic_index_in_dim(ordinal, device, 0, keepdims=False)
    gap = (device - my_owners + devices) % devices
    step_of = jnp.where(gap <= REACH, gap, gap - devices)
    cap_ids = jnp.arange(capacity, dtype=jnp.int32)
    my_local = lax.dynamic_index_in_dim(local_all, device, 0, keepdims=False)
    step_table = step_of + REACH
    index_table = jnp.where(step_of == 0, my_local, my_rank)
    step_ids = jnp.arange(span, dtype=jnp.int32)
    per_step = jnp.sum(step_table[None, :] == step_ids[:, None], axis=1)
    bounds = jnp.concatenate([jnp.zeros((1,), jnp.int32), jnp.cumsum(per_step)]).astype(jnp.int32)
    entry_ids = jnp.arange(slot_count, dtype=jnp.int32)
    same_before = jnp.sum(
        (step_table[None, :] == step_table[:, None]) & (entry_ids[None, :] < entry_ids[:, None]),
        axis=1,
    )
    position = bounds[step_table] + same_before
    entry_order = jnp.sum(
        jnp.where(position[None, :] == entry_ids[:, None], entry_ids[None, :], 0), axis=1
    ).astype(jnp.int32)
    pickers = []
    targets = []
    for step in range(-REACH, REACH + 1):
        if step == 0:
            continue
        reader = (device + step + devices) % devices
        reader_owners = lax.dynamic_index_in_dim(owners, reader, 0, keepdims=False)
        reader_rank = lax.dynamic_index_in_dim(ordinal, reader, 0, keepdims=False)
        reader_local = lax.dynamic_index_in_dim(local_all, reader, 0, keepdims=False)
        chosen = (reader_owners == device)[None, :] & (reader_rank[None, :] == cap_ids[:, None])
        used = jnp.any(chosen, axis=1)
        picked = jnp.sum(jnp.where(chosen, reader_local[None, :], 0), axis=1)
        pickers.append(picked)
        targets.append(jnp.where(used, picked, -1))
    all_targets = jnp.concatenate(targets, axis=0)
    all_pickers = jnp.concatenate(pickers, axis=0)

    mine_listed = lax.dynamic_slice_in_dim(neighbours, device * per_device, per_device, 0)
    block_ids = jnp.arange(order.shape[0], dtype=jnp.int32)
    nbr_order = jnp.sum(jnp.where(mine_listed[:, :, None] == block_ids, order, 0), axis=2)
    own_order = lax.dynamic_slice_in_dim(order, device * per_device, per_device, 0)
    usable = nbr_order < own_order[:, None]
    masked = jnp.where(usable[:, :, None, None], coeffs, jnp.zeros((), jnp.bfloat16))
    wide = jnp.transpose(masked, (0, 2, 1, 3)).reshape(per_device, block_size, slot_count // per_device * block_size)
    wide_t = jnp.swapaxes(masked, 2, 3).reshape(per_device, slot_count // per_device * block_size, block_size)
    inv_t = jnp.swapaxes(inv_factors, 1, 2)

    width = storm_cols // CHUNKS
    whitened_parts = []
    product_parts = []
    for chunk in range(CHUNKS):
        rows = storm_cov[chunk * width : (chunk + 1) * width]
        mixed = None
        for owner, shard in shards:
            cov_part = lax.dynamic_slice_in_dim(
                rows, owner * shard.shape[1], shard.shape[1], axis=1
            )
            term = lax.dot_general(
                shard, cov_part, (((1,), (1,)), ((), ())), preferred_element_type=jnp.float32
            )
            mixed = term if mixed is None else mixed + term
        mixed = mixed.astype(jnp.bfloat16)
        own_blocks = mixed.reshape(per_device, block_size, width)
        outgoing = pick(all_pickers, own_blocks, capacity, 2 * REACH)
        sources = []
        for k, step in enumerate([s for s in range(-REACH, REACH + 1) if s != 0]):
            sources.append(from_behind(outgoing[k], "blk", step))
        sources.insert(REACH, own_blocks)
        outs = local_stage(
            bounds, entry_order, index_table, sources, wide, wide_t, inv_factors, inv_t
        )
        whitened, total = outs[0], outs[1]
        backs = []
        for k, step in enumerate([s for s in range(-REACH, REACH + 1) if s != 0]):
            backs.append(from_behind(outs[2 + k], "blk", -step))
        product = accumulate(all_targets, total, backs)
        whitened_parts.append(whitened.reshape(node_rows, width))
        product_parts.append(product.reshape(node_rows, width))
    if CHUNKS == 1:
        return whitened_parts[0], product_parts[0]
    return jnp.concatenate(whitened_parts, axis=1), jnp.concatenate(product_parts, axis=1)


def solution(mesh):
    in_specs = (
        P("blk", "st"),
        P("st", None),
        P(),
        P(),
        P("blk", None, None, None),
        P("blk", None, None),
    )
    out_specs = (P("blk", "st"), P("blk", "st"))
    return jax.shard_map(local, mesh=mesh, in_specs=in_specs, out_specs=out_specs, check_vma=False)
```

```python
import jax
import jax.numpy as jnp
from jax import lax
from jax.experimental import pallas as pl
from jax.experimental.pallas import tpu as pltpu
from jax.sharding import PartitionSpec as P

REACH = 3
CHUNKS = 2


def from_behind(array, axis, by):
    count = lax.axis_size(axis)
    return lax.ppermute(array, axis, [(i, (i + by) % count) for i in range(count)])


def pick_kernel(table_ref, own_ref, *pieces):
    capacity = pieces[0].shape[0]
    for k, piece in enumerate(pieces):

        def body(slot, carry, k=k, piece=piece):
            piece[slot] = own_ref[table_ref[k * capacity + slot]]
            return carry

        lax.fori_loop(0, capacity, body, 0)


def pick(table, own, capacity, count):
    blocks, rows, width = own.shape
    vmem = pl.BlockSpec(memory_space=pltpu.VMEM)
    return pl.pallas_call(
        pick_kernel,
        out_shape=[jax.ShapeDtypeStruct((capacity, rows, width), own.dtype)] * count,
        in_specs=[pl.BlockSpec(memory_space=pltpu.SMEM), vmem],
        out_specs=[vmem] * count,
        cost_estimate=pl.CostEstimate(
            flops=0,
            bytes_accessed=2 * own.size + 2 * count * capacity * rows * width,
            transcendentals=0,
        ),
    )(table, own)


def local_kernel(bounds_ref, entry_ref, index_ref, *refs):
    sources = list(refs[:7])
    wide_ref, wide_t_ref, inv_ref, inv_t_ref = refs[7:11]
    whitened_ref, total_ref = refs[11:13]
    pieces = list(refs[13:19])
    pieces.insert(3, None)
    near_ref, half_ref, returned_ref = refs[19:22]
    own_ref = sources[3]
    blocks, rows, _ = own_ref.shape
    span = wide_ref.shape[2]

    for k, source in enumerate(sources):

        def fetch(position, carry, source=source):
            entry = entry_ref[position]
            start = pl.multiple_of(entry * rows, rows)
            near_ref[pl.ds(start, rows)] = source[index_ref[entry]]
            return carry

        lax.fori_loop(bounds_ref[k], bounds_ref[k + 1], fetch, 0)

    def condition(block, carry):
        start = pl.multiple_of(block * span, span)
        pulled = jnp.dot(
            wide_ref[block], near_ref[pl.ds(start, span)], preferred_element_type=jnp.float32
        )
        conditioned = (own_ref[block].astype(jnp.float32) - pulled).astype(jnp.bfloat16)
        whitened = jnp.dot(
            inv_ref[block], conditioned, preferred_element_type=jnp.float32
        ).astype(jnp.bfloat16)
        whitened_ref[block] = whitened
        lifted = jnp.dot(inv_t_ref[block], whitened, preferred_element_type=jnp.float32)
        total_ref[block] = lifted
        half_ref[block] = lifted.astype(jnp.bfloat16)
        return carry

    lax.fori_loop(0, blocks, condition, 0)

    def give_back(block, carry):
        start = pl.multiple_of(block * span, span)
        returned_ref[pl.ds(start, span)] = (
            -jnp.dot(wide_t_ref[block], half_ref[block], preferred_element_type=jnp.float32)
        ).astype(jnp.bfloat16)
        return carry

    lax.fori_loop(0, blocks, give_back, 0)

    for k, piece in enumerate(pieces):

        def store(position, carry, piece=piece):
            entry = entry_ref[position]
            index = index_ref[entry]
            start = pl.multiple_of(entry * rows, rows)
            part = returned_ref[pl.ds(start, rows)]
            if piece is None:
                total_ref[index] = total_ref[index] + part.astype(jnp.float32)
            else:
                piece[index] = part
            return carry

        lax.fori_loop(bounds_ref[k], bounds_ref[k + 1], store, 0)


def local_stage(bounds, entry_order, index_table, sources, masked, masked_t, inv, inv_t):
    own = sources[3]
    blocks, rows, width = own.shape
    piece_shape = sources[0].shape
    entries = masked.shape[0] * masked.shape[2] // rows
    vmem = pl.BlockSpec(memory_space=pltpu.VMEM)
    smem = pl.BlockSpec(memory_space=pltpu.SMEM)
    return pl.pallas_call(
        local_kernel,
        out_shape=[
            jax.ShapeDtypeStruct(own.shape, jnp.bfloat16),
            jax.ShapeDtypeStruct(own.shape, jnp.float32),
        ]
        + [jax.ShapeDtypeStruct(piece_shape, jnp.bfloat16)] * 6,
        in_specs=[smem, smem, smem] + [vmem] * 11,
        out_specs=[vmem] * 8,
        scratch_shapes=[
            pltpu.VMEM((entries * rows, width), jnp.bfloat16),
            pltpu.VMEM(own.shape, jnp.bfloat16),
            pltpu.VMEM((entries * rows, width), jnp.bfloat16),
        ],
        compiler_params=pltpu.CompilerParams(vmem_limit_bytes=56 * 1024 * 1024),
        cost_estimate=pl.CostEstimate(
            flops=2 * rows * rows * width * (2 * entries + 2 * blocks),
            bytes_accessed=2 * (2 * own.size + 12 * sources[0].size) + 8 * own.size,
            transcendentals=0,
        ),
    )(bounds, entry_order, index_table, *sources, masked, masked_t, inv, inv_t)


def accumulate_kernel(target_ref, lifted_ref, *refs):
    pieces = refs[:6]
    out_ref, total_ref = refs[6:8]
    capacity = pieces[0].shape[0]
    total_ref[...] = lifted_ref[...]
    for k, piece in enumerate(pieces):

        def body(slot, carry, k=k, piece=piece):
            target = target_ref[k * capacity + slot]

            @pl.when(target >= 0)
            def _():
                total_ref[target] = total_ref[target] + piece[slot].astype(jnp.float32)

            return carry

        lax.fori_loop(0, capacity, body, 0)
    out_ref[...] = total_ref[...].astype(out_ref.dtype)


def accumulate(target, total, pieces):
    blocks, rows, width = total.shape
    vmem = pl.BlockSpec(memory_space=pltpu.VMEM)
    return pl.pallas_call(
        accumulate_kernel,
        out_shape=jax.ShapeDtypeStruct(total.shape, jnp.bfloat16),
        in_specs=[pl.BlockSpec(memory_space=pltpu.SMEM), vmem] + [vmem] * 6,
        out_specs=vmem,
        scratch_shapes=[pltpu.VMEM(total.shape, jnp.float32)],
        compiler_params=pltpu.CompilerParams(vmem_limit_bytes=56 * 1024 * 1024),
        cost_estimate=pl.CostEstimate(
            flops=6 * pieces[0].size,
            bytes_accessed=6 * total.size + 12 * pieces[0].size,
            transcendentals=0,
        ),
    )(target, total, *pieces)


def local(field, storm_cov, order, neighbours, coeffs, inv_factors):
    node_rows, storm_cols = field.shape
    per_device, near_count, block_size, _ = coeffs.shape
    devices = lax.axis_size("blk")
    device = lax.axis_index("blk")
    slot_count = near_count * per_device
    span = 2 * REACH + 1
    capacity = (slot_count + span - 1) // span

    parts = lax.axis_size("st")
    part = lax.axis_index("st")
    if parts == 4:
        half = node_rows // 2
        top, bottom = field[:half], field[half:]
        right_top = from_behind(top, "st", -1)
        left_bottom = from_behind(bottom, "st", 1)
        left_top = from_behind(top, "st", 1)
        right_bottom = from_behind(bottom, "st", -1)
        far_top = from_behind(right_top, "st", -1)
        far_bottom = from_behind(left_bottom, "st", 1)
        left, right, far = (part + parts - 1) % parts, (part + 1) % parts, (part + 2) % parts
        halves = [
            [(part, top), (left, left_top), (right, right_top), (far, far_top)],
            [(part, bottom), (left, left_bottom), (right, right_bottom), (far, far_bottom)],
        ]
    else:
        halves = [[(0, lax.all_gather(field, "st", axis=1, tiled=True))]]

    listed = neighbours.reshape(devices, slot_count)
    owners = listed // per_device
    local_all = listed - owners * per_device
    earlier = jnp.tril(jnp.ones((slot_count, slot_count), jnp.bool_), -1)
    same_owner = owners[:, :, None] == owners[:, None, :]
    ordinal = jnp.sum(same_owner & earlier[None], axis=2)
    my_owners = lax.dynamic_index_in_dim(owners, device, 0, keepdims=False)
    my_rank = lax.dynamic_index_in_dim(ordinal, device, 0, keepdims=False)
    gap = (device - my_owners + devices) % devices
    step_of = jnp.where(gap <= REACH, gap, gap - devices)
    cap_ids = jnp.arange(capacity, dtype=jnp.int32)
    my_local = lax.dynamic_index_in_dim(local_all, device, 0, keepdims=False)
    step_table = step_of + REACH
    index_table = jnp.where(step_of == 0, my_local, my_rank)
    step_ids = jnp.arange(span, dtype=jnp.int32)
    per_step = jnp.sum(step_table[None, :] == step_ids[:, None], axis=1)
    bounds = jnp.concatenate([jnp.zeros((1,), jnp.int32), jnp.cumsum(per_step)]).astype(jnp.int32)
    entry_ids = jnp.arange(slot_count, dtype=jnp.int32)
    same_before = jnp.sum(
        (step_table[None, :] == step_table[:, None]) & (entry_ids[None, :] < entry_ids[:, None]),
        axis=1,
    )
    position = bounds[step_table] + same_before
    entry_order = jnp.sum(
        jnp.where(position[None, :] == entry_ids[:, None], entry_ids[None, :], 0), axis=1
    ).astype(jnp.int32)
    pickers = []
    targets = []
    for step in range(-REACH, REACH + 1):
        if step == 0:
            continue
        reader = (device + step + devices) % devices
        reader_owners = lax.dynamic_index_in_dim(owners, reader, 0, keepdims=False)
        reader_rank = lax.dynamic_index_in_dim(ordinal, reader, 0, keepdims=False)
        reader_local = lax.dynamic_index_in_dim(local_all, reader, 0, keepdims=False)
        chosen = (reader_owners == device)[None, :] & (reader_rank[None, :] == cap_ids[:, None])
        used = jnp.any(chosen, axis=1)
        picked = jnp.sum(jnp.where(chosen, reader_local[None, :], 0), axis=1)
        pickers.append(picked)
        targets.append(jnp.where(used, picked, -1))
    all_targets = jnp.concatenate(targets, axis=0)
    all_pickers = jnp.concatenate(pickers, axis=0)

    mine_listed = lax.dynamic_slice_in_dim(neighbours, device * per_device, per_device, 0)
    block_ids = jnp.arange(order.shape[0], dtype=jnp.int32)
    nbr_order = jnp.sum(jnp.where(mine_listed[:, :, None] == block_ids, order, 0), axis=2)
    own_order = lax.dynamic_slice_in_dim(order, device * per_device, per_device, 0)
    usable = nbr_order < own_order[:, None]
    masked = jnp.where(usable[:, :, None, None], coeffs, jnp.zeros((), jnp.bfloat16))
    wide = jnp.transpose(masked, (0, 2, 1, 3)).reshape(per_device, block_size, slot_count // per_device * block_size)
    wide_t = jnp.swapaxes(masked, 2, 3).reshape(per_device, slot_count // per_device * block_size, block_size)
    inv_t = jnp.swapaxes(inv_factors, 1, 2)

    width = storm_cols // CHUNKS
    whitened_parts = []
    product_parts = []
    for chunk in range(CHUNKS):
        rows = storm_cov[chunk * width : (chunk + 1) * width]
        mixed_halves = []
        for shards in halves:
            mixed = None
            for owner, shard in shards:
                cov_part = lax.dynamic_slice_in_dim(
                    rows, owner * shard.shape[1], shard.shape[1], axis=1
                )
                term = lax.dot_general(
                    shard, cov_part, (((1,), (1,)), ((), ())), preferred_element_type=jnp.float32
                )
                mixed = term if mixed is None else mixed + term
            mixed_halves.append(mixed.astype(jnp.bfloat16))
        mixed = jnp.concatenate(mixed_halves, axis=0)
        own_blocks = mixed.reshape(per_device, block_size, width)
        outgoing = pick(all_pickers, own_blocks, capacity, 2 * REACH)
        sources = []
        for k, step in enumerate([s for s in range(-REACH, REACH + 1) if s != 0]):
            sources.append(from_behind(outgoing[k], "blk", step))
        sources.insert(REACH, own_blocks)
        outs = local_stage(
            bounds, entry_order, index_table, sources, wide, wide_t, inv_factors, inv_t
        )
        whitened, total = outs[0], outs[1]
        backs = []
        for k, step in enumerate([s for s in range(-REACH, REACH + 1) if s != 0]):
            backs.append(from_behind(outs[2 + k], "blk", -step))
        product = accumulate(all_targets, total, backs)
        whitened_parts.append(whitened.reshape(node_rows, width))
        product_parts.append(product.reshape(node_rows, width))
    if CHUNKS == 1:
        return whitened_parts[0], product_parts[0]
    return jnp.concatenate(whitened_parts, axis=1), jnp.concatenate(product_parts, axis=1)


def solution(mesh):
    in_specs = (
        P("blk", "st"),
        P("st", None),
        P(),
        P(),
        P("blk", None, None, None),
        P("blk", None, None),
    )
    out_specs = (P("blk", "st"), P("blk", "st"))
    return jax.shard_map(local, mesh=mesh, in_specs=in_specs, out_specs=out_specs, check_vma=False)
```

```python
import jax
import jax.numpy as jnp
from jax import lax
from jax.experimental import pallas as pl
from jax.experimental.pallas import tpu as pltpu
from jax.sharding import PartitionSpec as P

REACH = 3
CHUNKS = 2


def from_behind(array, axis, by):
    count = lax.axis_size(axis)
    return lax.ppermute(array, axis, [(i, (i + by) % count) for i in range(count)])


def pick_kernel(table_ref, own_ref, *pieces):
    capacity = pieces[0].shape[0]
    for k, piece in enumerate(pieces):

        def body(slot, carry, k=k, piece=piece):
            piece[slot] = own_ref[table_ref[k * capacity + slot]]
            return carry

        lax.fori_loop(0, capacity, body, 0)


def pick(table, own, capacity, count):
    blocks, rows, width = own.shape
    vmem = pl.BlockSpec(memory_space=pltpu.VMEM)
    return pl.pallas_call(
        pick_kernel,
        out_shape=[jax.ShapeDtypeStruct((capacity, rows, width), own.dtype)] * count,
        in_specs=[pl.BlockSpec(memory_space=pltpu.SMEM), vmem],
        out_specs=[vmem] * count,
        cost_estimate=pl.CostEstimate(
            flops=0,
            bytes_accessed=2 * own.size + 2 * count * capacity * rows * width,
            transcendentals=0,
        ),
    )(table, own)


def local_kernel(bounds_ref, entry_ref, index_ref, *refs):
    sources = list(refs[:7])
    wide_ref, wide_t_ref, inv_ref, inv_t_ref = refs[7:11]
    whitened_ref, total_ref = refs[11:13]
    pieces = list(refs[13:19])
    pieces.insert(3, None)
    near_ref, half_ref, returned_ref = refs[19:22]
    own_ref = sources[3]
    blocks, rows, _ = own_ref.shape
    span = wide_ref.shape[2]

    for k, source in enumerate(sources):

        def fetch(position, carry, source=source):
            entry = entry_ref[position]
            start = pl.multiple_of(entry * rows, rows)
            near_ref[pl.ds(start, rows)] = source[index_ref[entry]]
            return carry

        lax.fori_loop(bounds_ref[k], bounds_ref[k + 1], fetch, 0)

    def condition(block, carry):
        start = pl.multiple_of(block * span, span)
        pulled = jnp.dot(
            wide_ref[block], near_ref[pl.ds(start, span)], preferred_element_type=jnp.float32
        )
        conditioned = (own_ref[block].astype(jnp.float32) - pulled).astype(jnp.bfloat16)
        whitened = jnp.dot(
            inv_ref[block], conditioned, preferred_element_type=jnp.float32
        ).astype(jnp.bfloat16)
        whitened_ref[block] = whitened
        lifted = jnp.dot(inv_t_ref[block], whitened, preferred_element_type=jnp.float32)
        total_ref[block] = lifted
        half_ref[block] = lifted.astype(jnp.bfloat16)
        return carry

    lax.fori_loop(0, blocks, condition, 0)

    def give_back(block, carry):
        start = pl.multiple_of(block * span, span)
        returned_ref[pl.ds(start, span)] = (
            -jnp.dot(wide_t_ref[block], half_ref[block], preferred_element_type=jnp.float32)
        ).astype(jnp.bfloat16)
        return carry

    lax.fori_loop(0, blocks, give_back, 0)

    for k, piece in enumerate(pieces):

        def store(position, carry, piece=piece):
            entry = entry_ref[position]
            index = index_ref[entry]
            start = pl.multiple_of(entry * rows, rows)
            part = returned_ref[pl.ds(start, rows)]
            if piece is None:
                total_ref[index] = total_ref[index] + part.astype(jnp.float32)
            else:
                piece[index] = part
            return carry

        lax.fori_loop(bounds_ref[k], bounds_ref[k + 1], store, 0)


def local_stage(bounds, entry_order, index_table, sources, masked, masked_t, inv, inv_t):
    own = sources[3]
    blocks, rows, width = own.shape
    piece_shape = sources[0].shape
    entries = masked.shape[0] * masked.shape[2] // rows
    vmem = pl.BlockSpec(memory_space=pltpu.VMEM)
    smem = pl.BlockSpec(memory_space=pltpu.SMEM)
    return pl.pallas_call(
        local_kernel,
        out_shape=[
            jax.ShapeDtypeStruct(own.shape, jnp.bfloat16),
            jax.ShapeDtypeStruct(own.shape, jnp.float32),
        ]
        + [jax.ShapeDtypeStruct(piece_shape, jnp.bfloat16)] * 6,
        in_specs=[smem, smem, smem] + [vmem] * 11,
        out_specs=[vmem] * 8,
        scratch_shapes=[
            pltpu.VMEM((entries * rows, width), jnp.bfloat16),
            pltpu.VMEM(own.shape, jnp.bfloat16),
            pltpu.VMEM((entries * rows, width), jnp.bfloat16),
        ],
        compiler_params=pltpu.CompilerParams(vmem_limit_bytes=56 * 1024 * 1024),
        cost_estimate=pl.CostEstimate(
            flops=2 * rows * rows * width * (2 * entries + 2 * blocks),
            bytes_accessed=2 * (2 * own.size + 12 * sources[0].size) + 8 * own.size,
            transcendentals=0,
        ),
    )(bounds, entry_order, index_table, *sources, masked, masked_t, inv, inv_t)


def accumulate_kernel(target_ref, lifted_ref, *refs):
    pieces = refs[:6]
    if len(refs) == 9:
        prev_ref = refs[6]
        out_ref, total_ref = refs[7:9]
    else:
        prev_ref = None
        out_ref, total_ref = refs[6:8]
    capacity = pieces[0].shape[0]
    total_ref[...] = lifted_ref[...]
    for k, piece in enumerate(pieces):

        def body(slot, carry, k=k, piece=piece):
            target = target_ref[k * capacity + slot]

            @pl.when(target >= 0)
            def _():
                total_ref[target] = total_ref[target] + piece[slot].astype(jnp.float32)

            return carry

        lax.fori_loop(0, capacity, body, 0)
    if prev_ref is None:
        out_ref[...] = total_ref[...].astype(out_ref.dtype)
    else:
        done = prev_ref.shape[2]
        out_ref[:, :, :done] = prev_ref[...]
        out_ref[:, :, done:] = total_ref[...].astype(out_ref.dtype)


def accumulate(target, total, pieces, prev=None):
    blocks, rows, width = total.shape
    done = 0 if prev is None else prev.shape[2]
    extra = [] if prev is None else [prev]
    vmem = pl.BlockSpec(memory_space=pltpu.VMEM)
    return pl.pallas_call(
        accumulate_kernel,
        out_shape=jax.ShapeDtypeStruct((blocks, rows, done + width), jnp.bfloat16),
        in_specs=[pl.BlockSpec(memory_space=pltpu.SMEM), vmem] + [vmem] * (6 + len(extra)),
        out_specs=vmem,
        scratch_shapes=[pltpu.VMEM(total.shape, jnp.float32)],
        compiler_params=pltpu.CompilerParams(vmem_limit_bytes=56 * 1024 * 1024),
        cost_estimate=pl.CostEstimate(
            flops=6 * pieces[0].size,
            bytes_accessed=6 * total.size + 12 * pieces[0].size,
            transcendentals=0,
        ),
    )(target, total, *pieces, *extra)


def local(field, storm_cov, order, neighbours, coeffs, inv_factors):
    node_rows, storm_cols = field.shape
    per_device, near_count, block_size, _ = coeffs.shape
    devices = lax.axis_size("blk")
    device = lax.axis_index("blk")
    slot_count = near_count * per_device
    span = 2 * REACH + 1
    capacity = (slot_count + span - 1) // span

    parts = lax.axis_size("st")
    part = lax.axis_index("st")
    if parts == 4:
        half = node_rows // 2
        from_left = from_behind(field, "st", 1)
        from_right = from_behind(field, "st", -1)
        far_top = from_behind(from_right[:half], "st", -1)
        far_bottom = from_behind(from_left[half:], "st", 1)
        shards = [
            (part, field),
            ((part + parts - 1) % parts, from_left),
            ((part + 1) % parts, from_right),
            ((part + 2) % parts, jnp.concatenate([far_top, far_bottom], axis=0)),
        ]
    else:
        field_all = lax.all_gather(field, "st", axis=1, tiled=True)
        shards = [(0, field_all)]

    listed = neighbours.reshape(devices, slot_count)
    owners = listed // per_device
    local_all = listed - owners * per_device
    earlier = jnp.tril(jnp.ones((slot_count, slot_count), jnp.bool_), -1)
    same_owner = owners[:, :, None] == owners[:, None, :]
    ordinal = jnp.sum(same_owner & earlier[None], axis=2)
    my_owners = lax.dynamic_index_in_dim(owners, device, 0, keepdims=False)
    my_rank = lax.dynamic_index_in_dim(ordinal, device, 0, keepdims=False)
    gap = (device - my_owners + devices) % devices
    step_of = jnp.where(gap <= REACH, gap, gap - devices)
    cap_ids = jnp.arange(capacity, dtype=jnp.int32)
    my_local = lax.dynamic_index_in_dim(local_all, device, 0, keepdims=False)
    step_table = step_of + REACH
    index_table = jnp.where(step_of == 0, my_local, my_rank)
    step_ids = jnp.arange(span, dtype=jnp.int32)
    per_step = jnp.sum(step_table[None, :] == step_ids[:, None], axis=1)
    bounds = jnp.concatenate([jnp.zeros((1,), jnp.int32), jnp.cumsum(per_step)]).astype(jnp.int32)
    entry_ids = jnp.arange(slot_count, dtype=jnp.int32)
    same_before = jnp.sum(
        (step_table[None, :] == step_table[:, None]) & (entry_ids[None, :] < entry_ids[:, None]),
        axis=1,
    )
    position = bounds[step_table] + same_before
    entry_order = jnp.sum(
        jnp.where(position[None, :] == entry_ids[:, None], entry_ids[None, :], 0), axis=1
    ).astype(jnp.int32)
    pickers = []
    targets = []
    for step in range(-REACH, REACH + 1):
        if step == 0:
            continue
        reader = (device + step + devices) % devices
        reader_owners = lax.dynamic_index_in_dim(owners, reader, 0, keepdims=False)
        reader_rank = lax.dynamic_index_in_dim(ordinal, reader, 0, keepdims=False)
        reader_local = lax.dynamic_index_in_dim(local_all, reader, 0, keepdims=False)
        chosen = (reader_owners == device)[None, :] & (reader_rank[None, :] == cap_ids[:, None])
        used = jnp.any(chosen, axis=1)
        picked = jnp.sum(jnp.where(chosen, reader_local[None, :], 0), axis=1)
        pickers.append(picked)
        targets.append(jnp.where(used, picked, -1))
    all_targets = jnp.concatenate(targets, axis=0)
    all_pickers = jnp.concatenate(pickers, axis=0)

    mine_listed = lax.dynamic_slice_in_dim(neighbours, device * per_device, per_device, 0)
    block_ids = jnp.arange(order.shape[0], dtype=jnp.int32)
    nbr_order = jnp.sum(jnp.where(mine_listed[:, :, None] == block_ids, order, 0), axis=2)
    own_order = lax.dynamic_slice_in_dim(order, device * per_device, per_device, 0)
    usable = nbr_order < own_order[:, None]
    masked = jnp.where(usable[:, :, None, None], coeffs, jnp.zeros((), jnp.bfloat16))
    wide = jnp.transpose(masked, (0, 2, 1, 3)).reshape(per_device, block_size, slot_count // per_device * block_size)
    wide_t = jnp.swapaxes(masked, 2, 3).reshape(per_device, slot_count // per_device * block_size, block_size)
    inv_t = jnp.swapaxes(inv_factors, 1, 2)

    width = storm_cols // CHUNKS
    whitened_parts = []
    product = None
    for chunk in range(CHUNKS):
        rows = storm_cov[chunk * width : (chunk + 1) * width]
        mixed = None
        for owner, shard in shards:
            cov_part = lax.dynamic_slice_in_dim(
                rows, owner * shard.shape[1], shard.shape[1], axis=1
            )
            term = lax.dot_general(
                shard, cov_part, (((1,), (1,)), ((), ())), preferred_element_type=jnp.float32
            )
            mixed = term if mixed is None else mixed + term
        mixed = mixed.astype(jnp.bfloat16)
        own_blocks = mixed.reshape(per_device, block_size, width)
        outgoing = pick(all_pickers, own_blocks, capacity, 2 * REACH)
        sources = []
        for k, step in enumerate([s for s in range(-REACH, REACH + 1) if s != 0]):
            sources.append(from_behind(outgoing[k], "blk", step))
        sources.insert(REACH, own_blocks)
        outs = local_stage(
            bounds, entry_order, index_table, sources, wide, wide_t, inv_factors, inv_t
        )
        whitened, total = outs[0], outs[1]
        backs = []
        for k, step in enumerate([s for s in range(-REACH, REACH + 1) if s != 0]):
            backs.append(from_behind(outs[2 + k], "blk", -step))
        product = accumulate(all_targets, total, backs, product)
        whitened_parts.append(whitened.reshape(node_rows, width))
    product = product.reshape(node_rows, storm_cols)
    if CHUNKS == 1:
        return whitened_parts[0], product
    return jnp.concatenate(whitened_parts, axis=1), product


def solution(mesh):
    in_specs = (
        P("blk", "st"),
        P("st", None),
        P(),
        P(),
        P("blk", None, None, None),
        P("blk", None, None),
    )
    out_specs = (P("blk", "st"), P("blk", "st"))
    return jax.shard_map(local, mesh=mesh, in_specs=in_specs, out_specs=out_specs, check_vma=False)
```
